256 devices in a mesh: group: 8 (over y_lo, x), dev: 32 (over z, y_hi, core).
Axes of the slice: x: 4, y: 4 (y_hi: 2, y_lo: 2; y = y_hi * 2 + y_lo), z: 8, core: 2. Of those that a mesh axis runs over, the one named last changes fastest.
Arguments:
- inputs: bfloat16 [8, 2048, 1024], P('group', 'dev'), may hold values from -6 to 6
- request: int32 [8, 2048], P('group'), may hold values from 0 to 63, never falling along the last dimension, each value on 1 to 64 neighbouring positions
- prefix_cache: bfloat16 [8, 6144, 2048], P('group', 'dev'), may hold values from -900 to 900
- norm1_gain: float32 [1024], replicated, may hold values from 0.5 to 1.5
- w_qkv: bfloat16 [1024, 3072], P(None, 'group'), may hold values from -0.375 to 0.375
- w_out: bfloat16 [1024, 1024], replicated, may hold values from -0.1875 to 0.1875
- norm2_gain: float32 [1024], replicated, may hold values from 0.5 to 1.5
- w_gate: bfloat16 [1024, 2816], P(None, 'group'), may hold values from -0.1875 to 0.1875
- w_up: bfloat16 [1024, 2816], P(None, 'group'), may hold values from -0.1875 to 0.1875
- w_down: bfloat16 [2816, 1024], P('group'), may hold values from -0.15625 to 0.15625
- norm3_gain: float32 [1024], replicated, may hold values from 0.5 to 1.5
- w_next: bfloat16 [1024, 3072], P(None, 'group'), may hold values from -0.1875 to 0.1875
Outputs:
- attended: bfloat16 [8, 2048, 1024], P('group', 'dev')
- layer_out: bfloat16 [8, 2048, 1024], P('group', 'dev')
- next_qkv: bfloat16 [8, 2048, 3072], P('group', 'dev')
The draws below stay inside these ranges and needn't reach their ends.
Inputs may be any that keep to these rules, and one draw needn't show every extreme that they name: A request's tokens are consecutive within its group; a request has at most 64 tokens, and some request has exactly 64.
All inputs are finite; a program needn't handle non-finite values.
Results may differ from the reference program's by a relative error of at most 0.01555.
The reference program's roundings to bfloat16 on the way (of `normed_in`, `projected`, `rounded`, `after_attn` and `hidden`) count: a program that leaves them out, or rounds other values in their place, can miss the bound.
Values may be sent and summed in bfloat16 or wider, within the bound.
No kernel may reach another device: no remote copies, remote signals or barrier semaphores. Data moves between devices by JAX's collectives and lax.ppermute only.
A program may use at most 128 MiB of HBM per device.

```python
import math
import jax
import jax.numpy as jnp
import numpy as np
from jax import lax

D = 1024
HEADS = 16
FF = 2816
TOK_DEV = 64
GROUPS = 8
SUF = 2048
PREFIX = 6144
REQS = 64


def draw_prefix_cache(key, part):
    first, second = jax.random.split(key, 2)
    full_shape = (GROUPS, PREFIX, D)
    key_part = 1.5 * jax.random.normal(first, full_shape, jnp.float32)
    value_part = 1.5 * jax.random.normal(second, full_shape, jnp.float32)
    key_part = jnp.clip(key_part, -900.0, 900.0)
    return jnp.concatenate([key_part, value_part], axis=-1).astype(jnp.bfloat16)


def with_spikes(result, own_key, source, target, shards_of, factor):
    owner, partner = [(jnp.arange(result.shape[dim]) // (result.shape[dim] // shards_of)).reshape([-1 if axis == dim else 1 for axis in range(result.ndim)]) for dim in (source, target)]
    chosen = jax.random.permutation(own_key, shards_of)[partner]
    strong = (owner == chosen) | (owner == (partner + shards_of // 2) % shards_of)
    return jnp.where(strong, factor * result, result)


def level_of(key, extent, pieces, least, high):
    def one(position, parts):
        draws = jax.random.uniform(jax.random.fold_in(jax.random.fold_in(key, 6), position), (parts,), jnp.float32, least / len(pieces), high / len(pieces))
        return jnp.repeat(jnp.exp(draws), extent[position] // parts).reshape((-1,) + (1,) * (len(extent) - position - 1))

    loudness = one(*pieces[0])
    for cut in pieces[1:]:
        loudness = loudness * one(*cut)
    return loudness


def split_up(count, total, most, skew):
    loads = [(1 << 20) // math.isqrt(grade ** skew) + 1 for grade in range(2, count + 1)]
    surplus, counts = total - most - (count - 1), [1] * (count - 1)
    while surplus > 0:
        free = [i for i in range(count - 1) if counts[i] < most]
        pool, budget = sum([loads[i] for i in free]), surplus
        for i in free:
            more = min(most - counts[i], max(1, budget * loads[i] // pool), surplus)
            counts[i] = counts[i] + more
            surplus = surplus - more
    return np.array([most] + counts)


def ragged(key, count, total, most, lean):
    if count == 2:
        one = jax.random.randint(key, (), max(1, total - most), min(most, total - 1) + 1)
        return jnp.stack([one, total - one])
    tallies = jnp.asarray(split_up(count, total, most, lean), jnp.int32)
    couples = (count - 1) // 2
    donor, sink = tallies[1:1 + 2 * couples:2], tallies[2:2 + 2 * couples:2]
    slack = jnp.minimum(donor - 1, most - sink)
    passed = jax.random.randint(jax.random.fold_in(key, 1), (couples,), 0, 1 << 20) % (slack + 1)
    tallies = tallies.at[1:1 + 2 * couples:2].set(donor - passed).at[2:2 + 2 * couples:2].set(sink + passed)
    return tallies[jax.random.permutation(jax.random.fold_in(key, 2), count)]


def bell_draw(own_key, extent, scale, bound, cuts=(), held_as=jnp.bfloat16):
    level = level_of(own_key, extent, cuts, -0.22, 0.18) if cuts else 1.0
    result = jax.random.normal(own_key, extent, jnp.float32) * scale * level
    return jnp.minimum(jnp.maximum(result, -bound), bound).astype(held_as)


def bell_draw_with(key, dims, deviation, limit, cuts, heavy, kind=jnp.bfloat16):
    values = deviation * jax.random.normal(key, dims, jnp.float32)
    if cuts:
        values = values * level_of(key, dims, cuts, -0.22, 0.18)
    return jnp.clip(with_spikes(values, jax.random.fold_in(key, 3), *heavy), -limit, limit).astype(kind)


def setup_inputs(seed: int = 0) -> dict:
    splits = jax.random.split(jax.random.key(seed), 13)
    return {
        "inputs": bell_draw(splits[0], (GROUPS, SUF, D), 1.0, 6.0, ((0, 8), (1, 32))),
        "request": jax.vmap(lambda own: jnp.searchsorted(jnp.cumsum(ragged(own, REQS, SUF, TOK_DEV, 2)), jnp.arange(SUF), side="right"))(jax.random.split(splits[1], GROUPS)).reshape((GROUPS, SUF)).astype(jnp.int32),
        "prefix_cache": draw_prefix_cache(jax.random.fold_in(splits[12], 71), 0),
        "norm1_gain": jnp.clip(1.0 + 0.1 * jax.random.normal(splits[3], (D,), jnp.float32), 0.5, 1.5),
        "w_qkv": bell_draw(splits[4], (D, 3 * D), (D // 4) ** -0.5, 0.375, ((1, 8),)),
        "w_out": bell_draw(splits[5], (D, D), D ** -0.5, 0.1875),
        "norm2_gain": jnp.clip(1.0 + 0.1 * jax.random.normal(splits[6], (D,), jnp.float32), 0.5, 1.5),
        "w_gate": bell_draw(splits[7], (D, FF), D ** -0.5, 0.1875, ((1, 8),)),
        "w_up": bell_draw(splits[8], (D, FF), D ** -0.5, 0.1875, ((1, 8),)),
        "w_down": bell_draw_with(splits[9], (FF, D), FF ** -0.5, 0.15625, ((0, 8),), (0, 1, 8, 2.0)),
        "norm3_gain": jnp.clip(1.0 + 0.1 * jax.random.normal(splits[10], (D,), jnp.float32), 0.5, 1.5),
        "w_next": bell_draw(splits[11], (D, 3 * D), D ** -0.5, 0.1875, ((1, 8),)),
    }


NORM_EPSILON = 1e-05

def rms_norm(values, gain):
    wide = values.astype(jnp.float32)
    factor = lax.rsqrt(lax.optimization_barrier(jnp.mean(wide * wide, axis=-1, keepdims=True)) + NORM_EPSILON)
    return (wide * factor * gain).astype(jnp.bfloat16)

def one_group(group_inputs, group_requests, group_cache, weight_set):
    norm1_gain, w_qkv, w_out, norm2_gain, w_gate, w_up, w_down, norm3_gain, w_next = weight_set
    model_width = group_inputs.shape[1]
    head_count = HEADS
    head_size = model_width // head_count
    score_scale = 1.0 / math.sqrt(head_size)
    total_tokens = group_inputs.shape[0]
    prefix_len = group_cache.shape[0]
    normed_in = rms_norm(group_inputs, norm1_gain)
    projected = jnp.dot(normed_in, w_qkv, preferred_element_type=jnp.float32).astype(jnp.bfloat16)
    queries = projected[:, :model_width].reshape(total_tokens, head_count, head_size)
    all_keys = jnp.concatenate([group_cache[:, :model_width], projected[:, model_width:2 * model_width]], axis=0)
    all_values = jnp.concatenate([group_cache[:, model_width:], projected[:, 2 * model_width:]], axis=0)
    all_keys = all_keys.reshape(-1, head_count, head_size).astype(jnp.float32)
    all_values = all_values.reshape(-1, head_count, head_size).astype(jnp.float32)
    block_rows = TOK_DEV
    query_blocks = queries.reshape(total_tokens // block_rows, block_rows, head_count, head_size)
    request_blocks = group_requests.reshape(total_tokens // block_rows, block_rows)

    def attend(block):
        query_block, request_block = block
        scores = jnp.einsum('qhd,khd->hqk', query_block.astype(jnp.float32), all_keys) * score_scale
        same_request = request_block[:, None] == group_requests[None, :]
        allowed = jnp.concatenate([jnp.ones((block_rows, prefix_len), dtype=bool), same_request], axis=1)
        scores = jnp.where(allowed[None], scores, -jnp.inf)
        row_top = lax.optimization_barrier(jnp.max(scores, axis=-1, keepdims=True))
        weights_full = jnp.exp(scores - row_top)
        row_total = lax.optimization_barrier(jnp.sum(weights_full, axis=-1))
        rounded = lax.optimization_barrier(weights_full.astype(jnp.bfloat16)).astype(jnp.float32)
        mixed = jnp.einsum('hqk,khd->qhd', rounded, all_values)
        mixed = mixed / jnp.transpose(row_total)[:, :, None]
        return mixed.reshape(block_rows, model_width).astype(jnp.bfloat16)
    attended = lax.map(attend, (query_blocks, request_blocks)).reshape(total_tokens, model_width)
    after_attn = (group_inputs.astype(jnp.float32) + jnp.dot(attended, w_out, preferred_element_type=jnp.float32)).astype(jnp.bfloat16)
    normed_mid = rms_norm(after_attn, norm2_gain)
    gate_proj = jnp.dot(normed_mid, w_gate, preferred_element_type=jnp.float32)
    up_proj = jnp.dot(normed_mid, w_up, preferred_element_type=jnp.float32)
    hidden = (jax.nn.silu(gate_proj) * up_proj).astype(jnp.bfloat16)
    layer_out = (after_attn.astype(jnp.float32) + jnp.dot(hidden, w_down, preferred_element_type=jnp.float32)).astype(jnp.bfloat16)
    normed_out = rms_norm(layer_out, norm3_gain)
    next_qkv = jnp.dot(normed_out, w_next, preferred_element_type=jnp.float32).astype(jnp.bfloat16)
    return (attended, layer_out, next_qkv)

def reference(inputs, request, prefix_cache, norm1_gain, w_qkv, w_out, norm2_gain, w_gate, w_up, w_down, norm3_gain, w_next):
    weight_set = (norm1_gain, w_qkv, w_out, norm2_gain, w_gate, w_up, w_down, norm3_gain, w_next)
    attended, layer_out, next_qkv = lax.map(lambda item: one_group(item[0], item[1], item[2], weight_set), (inputs, request, prefix_cache))
    return (attended, layer_out, next_qkv)
```

```python
import math

import jax
import jax.numpy as jnp
from jax import lax
from jax.sharding import Mesh
from jax.sharding import PartitionSpec as P

HEADS = 16


NORM_EPSILON = 1e-05

CLASS = ("z", "yh")
DEV = ("z", "yh", "core")


def rms_norm(values, gain):
    wide = values.astype(jnp.float32)
    factor = lax.rsqrt(jnp.mean(wide * wide, axis=-1, keepdims=True) + NORM_EPSILON)
    return (wide * factor * gain).astype(jnp.bfloat16)


def gather_rows(values, handler):
    return handler(lax.all_gather(values, "group", axis=0, tiled=True), jnp.int32(0))


def return_rows(columns):
    return lax.all_to_all(columns, "group", split_axis=0, concat_axis=1, tiled=True)


def projector(weight):

    def apply_rows(portion, offset):
        return jnp.dot(portion, weight, preferred_element_type=jnp.float32).astype(jnp.bfloat16)

    return apply_rows


def head_attention(queries, query_ids, prefix_kv, suffix_kv, suffix_ids, score_scale):
    blocks, rows, head_size = queries.shape
    prefix_keys = prefix_kv[:, 0]
    prefix_values = prefix_kv[:, 1]
    prefix_scores = (
        jnp.einsum("bqd,kd->bqk", queries, prefix_keys, preferred_element_type=jnp.float32)
        * score_scale
    )
    near_scores = (
        jnp.einsum("bqd,bkd->bqk", queries, suffix_kv[:, :, 0], preferred_element_type=jnp.float32)
        * score_scale
    )
    allowed = query_ids[:, :, None] == suffix_ids[:, None, :]
    near_scores = jnp.where(allowed, near_scores, -jnp.inf)
    row_top = jnp.maximum(jnp.max(prefix_scores, axis=-1), jnp.max(near_scores, axis=-1))
    prefix_weights = jnp.exp(prefix_scores - row_top[:, :, None])
    near_weights = jnp.exp(near_scores - row_top[:, :, None])
    row_total = jnp.sum(prefix_weights, axis=-1) + jnp.sum(near_weights, axis=-1)
    mixed = jnp.einsum(
        "bqk,kd->bqd",
        prefix_weights.astype(jnp.bfloat16),
        prefix_values,
        preferred_element_type=jnp.float32,
    ) + jnp.einsum(
        "bqk,bkd->bqd",
        near_weights.astype(jnp.bfloat16),
        suffix_kv[:, :, 1],
        preferred_element_type=jnp.float32,
    )
    return (mixed / row_total[:, :, None]).astype(jnp.bfloat16)


def on_device(
    inputs,
    request,
    prefix_cache,
    norm1_gain,
    w_qkv,
    w_out,
    norm2_gain,
    w_gate,
    w_up,
    w_down,
    norm3_gain,
    w_next,
):
    tokens = inputs[0]
    tok_rows, model_width = tokens.shape
    head_count = HEADS
    head_size = model_width // head_count
    score_scale = 1.0 / math.sqrt(head_size)
    class_size = lax.axis_size(CLASS)
    core = lax.axis_index("core")
    normed_in = rms_norm(tokens, norm1_gain)
    projected = return_rows(gather_rows(normed_in, projector(w_qkv)))
    queries = projected[:, :model_width].reshape(tok_rows, head_count, head_size).transpose(1, 0, 2)
    suffix_kv = (
        projected[:, model_width:].reshape(tok_rows, 2, head_count, head_size).transpose(2, 0, 1, 3)
    )
    cache = prefix_cache[0]
    cache_rows = cache.shape[0]
    prefix_kv = cache.reshape(cache_rows, 2, head_count, head_size).transpose(2, 0, 1, 3)
    head_queries = lax.all_to_all(queries, CLASS, 0, 0, tiled=True)
    both_kv = jnp.concatenate([prefix_kv, suffix_kv], axis=1)
    class_kv = lax.all_to_all(both_kv, CLASS, 0, 0, tiled=True)
    partner_kv = lax.ppermute(class_kv, "core", [(0, 1), (1, 0)])
    pair = [class_kv, partner_kv]
    all_kv = jnp.stack([lax.select(core == 0, pair[0], pair[1]), lax.select(core == 0, pair[1], pair[0])], axis=1)
    dev_count = 2 * class_size
    all_kv = all_kv.reshape(dev_count, cache_rows + tok_rows, 2, head_size)
    group_prefix = all_kv[:, :cache_rows].reshape(dev_count * cache_rows, 2, head_size)
    group_suffix = all_kv[:, cache_rows:]
    group_requests = request[0].reshape(dev_count, tok_rows)
    pad_kv = jnp.zeros((1, tok_rows, 2, head_size), group_suffix.dtype)
    padded_suffix = jnp.concatenate([pad_kv, group_suffix, pad_kv], axis=0)
    pad_ids = jnp.full((1, tok_rows), -1, jnp.int32)
    padded_ids = jnp.concatenate([pad_ids, group_requests, pad_ids], axis=0)
    source = 2 * jnp.arange(class_size, dtype=jnp.int32) + core
    near = source[:, None] + jnp.arange(3, dtype=jnp.int32)[None, :]
    near_kv = jnp.take(padded_suffix, near, axis=0).reshape(class_size, 3 * tok_rows, 2, head_size)
    near_ids = jnp.take(padded_ids, near, axis=0).reshape(class_size, 3 * tok_rows)
    query_ids = jnp.take(group_requests, source, axis=0)
    chunks = 4
    per = class_size // chunks

    def attend(part):
        q, qi, nk, ni = part
        return head_attention(q, qi, group_prefix, nk, ni, score_scale)

    head_out = lax.map(
        attend,
        (
            head_queries.reshape(chunks, per, tok_rows, head_size),
            query_ids.reshape(chunks, per, tok_rows),
            near_kv.reshape(chunks, per, 3 * tok_rows, 2, head_size),
            near_ids.reshape(chunks, per, 3 * tok_rows),
        ),
    ).reshape(class_size, tok_rows, head_size)
    back = lax.all_to_all(head_out, CLASS, 0, 0, tiled=True)
    attended = back.transpose(1, 0, 2).reshape(tok_rows, model_width)
    after_attn = (
        tokens.astype(jnp.float32) + jnp.dot(attended, w_out, preferred_element_type=jnp.float32)
    ).astype(jnp.bfloat16)

    def expand(portion, offset):
        normed_mid = rms_norm(portion, norm2_gain)
        gate_proj = jnp.dot(normed_mid, w_gate, preferred_element_type=jnp.float32)
        up_proj = jnp.dot(normed_mid, w_up, preferred_element_type=jnp.float32)
        return (jax.nn.silu(gate_proj) * up_proj).astype(jnp.bfloat16)

    hidden = gather_rows(after_attn, expand)
    own_sums = lax.psum_scatter(
        jnp.dot(hidden, w_down, preferred_element_type=jnp.float32),
        "group",
        scatter_dimension=0,
        tiled=True,
    )
    layer_out = (after_attn.astype(jnp.float32) + own_sums).astype(jnp.bfloat16)
    next_qkv = return_rows(gather_rows(rms_norm(layer_out, norm3_gain), projector(w_next)))
    return (attended[None], layer_out[None], next_qkv[None])


def solution(mesh):
    group_count, dev_count = mesh.devices.shape
    fine = Mesh(
        mesh.devices.reshape(group_count, dev_count // 4, 2, 2), ("group", "z", "yh", "core")
    )
    in_specs = (
        P("group", DEV, None),
        P("group", None),
        P("group", DEV, None),
        P(),
        P(None, "group"),
        P(),
        P(),
        P(None, "group"),
        P(None, "group"),
        P("group", None),
        P(),
        P(None, "group"),
    )
    out_specs = (P("group", DEV, None), P("group", DEV, None), P("group", DEV, None))
    return jax.shard_map(
        on_device, mesh=fine, in_specs=in_specs, out_specs=out_specs, check_vma=False
    )
```

```python
import math

import jax
import jax.numpy as jnp
from jax import lax
from jax.sharding import Mesh
from jax.sharding import PartitionSpec as P

HEADS = 16


NORM_EPSILON = 1e-05

CLASS = ("z", "yh")
DEV = ("z", "yh", "core")


def rms_norm(values, gain):
    wide = values.astype(jnp.float32)
    factor = lax.rsqrt(jnp.mean(wide * wide, axis=-1, keepdims=True) + NORM_EPSILON)
    return (wide * factor * gain).astype(jnp.bfloat16)


def gather_rows(values, handler):
    count = lax.axis_size("group")
    copies = jnp.broadcast_to(values[None], (count,) + values.shape)
    gathered = lax.all_to_all(copies, "group", 0, 0, tiled=True)
    return handler(gathered.reshape(-1, values.shape[-1]), jnp.int32(0))


def scatter_sums(partial):
    count = lax.axis_size("group")
    pieces = partial.reshape(count, -1, partial.shape[-1])
    return jnp.sum(lax.all_to_all(pieces, "group", 0, 0, tiled=True), axis=0)


def return_rows(columns):
    return lax.all_to_all(columns, "group", split_axis=0, concat_axis=1, tiled=True)


def projector(weight):

    def apply_rows(portion, offset):
        return jnp.dot(portion, weight, preferred_element_type=jnp.float32).astype(jnp.bfloat16)

    return apply_rows


def head_attention(queries, query_ids, prefix_kv, suffix_kv, suffix_ids, score_scale):
    blocks, rows, head_size = queries.shape
    prefix_keys = prefix_kv[:, 0]
    prefix_values = prefix_kv[:, 1]
    prefix_scores = (
        jnp.einsum("bqd,kd->bqk", queries, prefix_keys, preferred_element_type=jnp.float32)
        * score_scale
    )
    near_scores = (
        jnp.einsum("bqd,bkd->bqk", queries, suffix_kv[:, :, 0], preferred_element_type=jnp.float32)
        * score_scale
    )
    allowed = query_ids[:, :, None] == suffix_ids[:, None, :]
    near_scores = jnp.where(allowed, near_scores, -jnp.inf)
    row_top = jnp.maximum(jnp.max(prefix_scores, axis=-1), jnp.max(near_scores, axis=-1))
    prefix_weights = jnp.exp(prefix_scores - row_top[:, :, None])
    near_weights = jnp.exp(near_scores - row_top[:, :, None])
    row_total = jnp.sum(prefix_weights, axis=-1) + jnp.sum(near_weights, axis=-1)
    mixed = jnp.einsum(
        "bqk,kd->bqd",
        prefix_weights.astype(jnp.bfloat16),
        prefix_values,
        preferred_element_type=jnp.float32,
    ) + jnp.einsum(
        "bqk,bkd->bqd",
        near_weights.astype(jnp.bfloat16),
        suffix_kv[:, :, 1],
        preferred_element_type=jnp.float32,
    )
    return (mixed / row_total[:, :, None]).astype(jnp.bfloat16)


def on_device(
    inputs,
    request,
    prefix_cache,
    norm1_gain,
    w_qkv,
    w_out,
    norm2_gain,
    w_gate,
    w_up,
    w_down,
    norm3_gain,
    w_next,
):
    tokens = inputs[0]
    tok_rows, model_width = tokens.shape
    head_count = HEADS
    head_size = model_width // head_count
    score_scale = 1.0 / math.sqrt(head_size)
    class_size = lax.axis_size(CLASS)
    core = lax.axis_index("core")
    normed_in = rms_norm(tokens, norm1_gain)
    projected = return_rows(gather_rows(normed_in, projector(w_qkv)))
    queries = projected[:, :model_width].reshape(tok_rows, head_count, head_size).transpose(1, 0, 2)
    suffix_kv = (
        projected[:, model_width:].reshape(tok_rows, 2, head_count, head_size).transpose(2, 0, 1, 3)
    )
    cache = prefix_cache[0]
    cache_rows = cache.shape[0]
    prefix_kv = cache.reshape(cache_rows, 2, head_count, head_size).transpose(2, 0, 1, 3)
    head_queries = lax.all_to_all(queries, CLASS, 0, 0, tiled=True)
    both_kv = jnp.concatenate([prefix_kv, suffix_kv], axis=1)
    class_kv = lax.all_to_all(both_kv, CLASS, 0, 0, tiled=True)
    partner_kv = lax.ppermute(class_kv, "core", [(0, 1), (1, 0)])
    pair = [class_kv, partner_kv]
    all_kv = jnp.stack([lax.select(core == 0, pair[0], pair[1]), lax.select(core == 0, pair[1], pair[0])], axis=1)
    dev_count = 2 * class_size
    all_kv = all_kv.reshape(dev_count, cache_rows + tok_rows, 2, head_size)
    group_prefix = all_kv[:, :cache_rows].reshape(dev_count * cache_rows, 2, head_size)
    group_suffix = all_kv[:, cache_rows:]
    group_requests = request[0].reshape(dev_count, tok_rows)
    pad_kv = jnp.zeros((1, tok_rows, 2, head_size), group_suffix.dtype)
    padded_suffix = jnp.concatenate([pad_kv, group_suffix, pad_kv], axis=0)
    pad_ids = jnp.full((1, tok_rows), -1, jnp.int32)
    padded_ids = jnp.concatenate([pad_ids, group_requests, pad_ids], axis=0)
    source = 2 * jnp.arange(class_size, dtype=jnp.int32) + core
    near = source[:, None] + jnp.arange(3, dtype=jnp.int32)[None, :]
    near_kv = jnp.take(padded_suffix, near, axis=0).reshape(class_size, 3 * tok_rows, 2, head_size)
    near_ids = jnp.take(padded_ids, near, axis=0).reshape(class_size, 3 * tok_rows)
    query_ids = jnp.take(group_requests, source, axis=0)
    chunks = 4
    per = class_size // chunks

    def attend(part):
        q, qi, nk, ni = part
        return head_attention(q, qi, group_prefix, nk, ni, score_scale)

    head_out = lax.map(
        attend,
        (
            head_queries.reshape(chunks, per, tok_rows, head_size),
            query_ids.reshape(chunks, per, tok_rows),
            near_kv.reshape(chunks, per, 3 * tok_rows, 2, head_size),
            near_ids.reshape(chunks, per, 3 * tok_rows),
        ),
    ).reshape(class_size, tok_rows, head_size)
    back = lax.all_to_all(head_out, CLASS, 0, 0, tiled=True)
    attended = back.transpose(1, 0, 2).reshape(tok_rows, model_width)
    after_attn = (
        tokens.astype(jnp.float32) + jnp.dot(attended, w_out, preferred_element_type=jnp.float32)
    ).astype(jnp.bfloat16)

    def expand(portion, offset):
        normed_mid = rms_norm(portion, norm2_gain)
        gate_proj = jnp.dot(normed_mid, w_gate, preferred_element_type=jnp.float32)
        up_proj = jnp.dot(normed_mid, w_up, preferred_element_type=jnp.float32)
        return (jax.nn.silu(gate_proj) * up_proj).astype(jnp.bfloat16)

    hidden = gather_rows(after_attn, expand)
    own_sums = scatter_sums(jnp.dot(hidden, w_down, preferred_element_type=jnp.float32))
    layer_out = (after_attn.astype(jnp.float32) + own_sums).astype(jnp.bfloat16)
    next_qkv = return_rows(gather_rows(rms_norm(layer_out, norm3_gain), projector(w_next)))
    return (attended[None], layer_out[None], next_qkv[None])


def solution(mesh):
    group_count, dev_count = mesh.devices.shape
    fine = Mesh(
        mesh.devices.reshape(group_count, dev_count // 4, 2, 2), ("group", "z", "yh", "core")
    )
    in_specs = (
        P("group", DEV, None),
        P("group", None),
        P("group", DEV, None),
        P(),
        P(None, "group"),
        P(),
        P(),
        P(None, "group"),
        P(None, "group"),
        P("group", None),
        P(),
        P(None, "group"),
    )
    out_specs = (P("group", DEV, None), P("group", DEV, None), P("group", DEV, None))
    return jax.shard_map(
        on_device, mesh=fine, in_specs=in_specs, out_specs=out_specs, check_vma=False
    )
```

```python
import math

import jax
import jax.numpy as jnp
from jax import lax
from jax.sharding import Mesh
from jax.sharding import PartitionSpec as P

HEADS = 16


NORM_EPSILON = 1e-05

CLASS = ("z", "yh")
DEV = ("z", "yh", "core")


def rms_norm(values, gain):
    wide = values.astype(jnp.float32)
    factor = lax.rsqrt(jnp.mean(wide * wide, axis=-1, keepdims=True) + NORM_EPSILON)
    return (wide * factor * gain).astype(jnp.bfloat16)


def gather_rows(values, handler):
    count = lax.axis_size("group")
    copies = jnp.broadcast_to(values[None], (count,) + values.shape)
    gathered = lax.all_to_all(copies, "group", 0, 0, tiled=True)
    return handler(gathered.reshape(-1, values.shape[-1]), jnp.int32(0))


def scatter_sums(partial):
    count = lax.axis_size("group")
    pieces = partial.reshape(count, -1, partial.shape[-1])
    return jnp.sum(lax.all_to_all(pieces, "group", 0, 0, tiled=True), axis=0)


def return_rows(columns):
    return lax.all_to_all(columns, "group", split_axis=0, concat_axis=1, tiled=True)


def projector(weight):

    def apply_rows(portion, offset):
        return jnp.dot(portion, weight, preferred_element_type=jnp.float32).astype(jnp.bfloat16)

    return apply_rows


def head_attention(queries, query_ids, prefix_keys, prefix_values, suffix_kv, suffix_ids, score_scale):
    prefix_scores = (
        jnp.einsum("bqd,kd->bqk", queries, prefix_keys, preferred_element_type=jnp.float32)
        * score_scale
    )
    near_scores = (
        jnp.einsum("bqd,bkd->bqk", queries, suffix_kv[:, :, 0], preferred_element_type=jnp.float32)
        * score_scale
    )
    allowed = query_ids[:, :, None] == suffix_ids[:, None, :]
    near_scores = jnp.where(allowed, near_scores, -jnp.inf)
    row_top = jnp.maximum(jnp.max(prefix_scores, axis=-1), jnp.max(near_scores, axis=-1))
    prefix_weights = jnp.exp(prefix_scores - row_top[:, :, None])
    near_weights = jnp.exp(near_scores - row_top[:, :, None])
    row_total = jnp.sum(prefix_weights, axis=-1) + jnp.sum(near_weights, axis=-1)
    mixed = jnp.einsum(
        "bqk,kd->bqd",
        prefix_weights.astype(jnp.bfloat16),
        prefix_values,
        preferred_element_type=jnp.float32,
    ) + jnp.einsum(
        "bqk,bkd->bqd",
        near_weights.astype(jnp.bfloat16),
        suffix_kv[:, :, 1],
        preferred_element_type=jnp.float32,
    )
    return (mixed / row_total[:, :, None]).astype(jnp.bfloat16)


def on_device(
    inputs,
    request,
    prefix_cache,
    norm1_gain,
    w_qkv,
    w_out,
    norm2_gain,
    w_gate,
    w_up,
    w_down,
    norm3_gain,
    w_next,
):
    tokens = inputs[0]
    tok_rows, model_width = tokens.shape
    head_count = HEADS
    head_size = model_width // head_count
    score_scale = 1.0 / math.sqrt(head_size)
    class_size = lax.axis_size(CLASS)
    core = lax.axis_index("core")
    cache = prefix_cache[0]
    cache_rows = cache.shape[0]
    prefix_kv = cache.reshape(cache_rows, 2, head_count, head_size).transpose(2, 1, 0, 3)
    class_prefix = lax.all_to_all(prefix_kv, CLASS, 0, 0, tiled=True)
    partner_prefix = lax.ppermute(class_prefix, "core", [(0, 1), (1, 0)])
    group_prefix = jnp.concatenate([class_prefix, partner_prefix], axis=0)
    prefix_keys = group_prefix[:, 0].reshape(-1, head_size)
    prefix_values = group_prefix[:, 1].reshape(-1, head_size)
    normed_in = rms_norm(tokens, norm1_gain)
    projected = return_rows(gather_rows(normed_in, projector(w_qkv)))
    own_qkv = projected.reshape(tok_rows, 3, head_count, head_size).transpose(2, 0, 1, 3)
    class_qkv = lax.all_to_all(own_qkv, CLASS, 0, 0, tiled=True)
    head_queries = class_qkv[:, :, 0]
    class_kv = class_qkv[:, :, 1:]
    partner_kv = lax.ppermute(class_kv, "core", [(0, 1), (1, 0)])
    pad_kv = jnp.zeros((1,) + partner_kv.shape[1:], partner_kv.dtype)
    padded_kv = jnp.concatenate([pad_kv, partner_kv, pad_kv], axis=0)
    before_kv = lax.dynamic_slice_in_dim(padded_kv, core, class_size, 0)
    after_kv = lax.dynamic_slice_in_dim(padded_kv, core + 1, class_size, 0)
    near_kv = jnp.concatenate([before_kv, class_kv, after_kv], axis=1)
    dev_ids = request[0].reshape(2 * class_size, tok_rows)
    pad_ids = jnp.full((1, tok_rows), -1, jnp.int32)
    padded_ids = jnp.concatenate([pad_ids, dev_ids, pad_ids], axis=0)
    window = lax.dynamic_slice_in_dim(padded_ids, core, 2 * class_size + 1, 0)
    query_ids = window[1::2]
    near_ids = jnp.concatenate([window[0:-1:2], query_ids, window[2::2]], axis=1)
    head_out = head_attention(
        head_queries, query_ids, prefix_keys, prefix_values, near_kv, near_ids, score_scale
    )
    back = lax.all_to_all(head_out, CLASS, 0, 0, tiled=True)
    attended = back.transpose(1, 0, 2).reshape(tok_rows, model_width)
    after_attn = (
        tokens.astype(jnp.float32) + jnp.dot(attended, w_out, preferred_element_type=jnp.float32)
    ).astype(jnp.bfloat16)

    def expand(portion, offset):
        normed_mid = rms_norm(portion, norm2_gain)
        gate_proj = jnp.dot(normed_mid, w_gate, preferred_element_type=jnp.float32)
        up_proj = jnp.dot(normed_mid, w_up, preferred_element_type=jnp.float32)
        return (jax.nn.silu(gate_proj) * up_proj).astype(jnp.bfloat16)

    hidden = gather_rows(after_attn, expand)
    own_sums = scatter_sums(jnp.dot(hidden, w_down, preferred_element_type=jnp.float32))
    layer_out = (after_attn.astype(jnp.float32) + own_sums).astype(jnp.bfloat16)
    next_qkv = return_rows(gather_rows(rms_norm(layer_out, norm3_gain), projector(w_next)))
    return (attended[None], layer_out[None], next_qkv[None])


def solution(mesh):
    group_count, dev_count = mesh.devices.shape
    fine = Mesh(
        mesh.devices.reshape(group_count, dev_count // 4, 2, 2), ("group", "z", "yh", "core")
    )
    in_specs = (
        P("group", DEV, None),
        P("group", None),
        P("group", DEV, None),
        P(),
        P(None, "group"),
        P(),
        P(),
        P(None, "group"),
        P(None, "group"),
        P("group", None),
        P(),
        P(None, "group"),
    )
    out_specs = (P("group", DEV, None), P("group", DEV, None), P("group", DEV, None))
    return jax.shard_map(
        on_device, mesh=fine, in_specs=in_specs, out_specs=out_specs, check_vma=False
    )
```

```python
import math

import jax
import jax.numpy as jnp
from jax import lax
from jax.sharding import Mesh
from jax.sharding import PartitionSpec as P

HEADS = 16


NORM_EPSILON = 1e-05

CLASS = ("z", "yh")
DEV = ("z", "yh", "core")


def rms_norm(values, gain):
    wide = values.astype(jnp.float32)
    factor = lax.rsqrt(jnp.mean(wide * wide, axis=-1, keepdims=True) + NORM_EPSILON)
    return (wide * factor * gain).astype(jnp.bfloat16)


def gather_rows(values, handler):
    count = lax.axis_size("group")
    copies = jnp.broadcast_to(values[None], (count,) + values.shape)
    gathered = lax.all_to_all(copies, "group", 0, 0, tiled=True)
    return handler(gathered.reshape(-1, values.shape[-1]), jnp.int32(0))


def scatter_sums(partial):
    count = lax.axis_size("group")
    pieces = partial.reshape(count, -1, partial.shape[-1])
    return jnp.sum(lax.all_to_all(pieces, "group", 0, 0, tiled=True), axis=0)


def return_rows(columns):
    return lax.all_to_all(columns, "group", split_axis=0, concat_axis=1, tiled=True)


def projector(weight):

    def apply_rows(portion, offset):
        return jnp.dot(portion, weight, preferred_element_type=jnp.float32).astype(jnp.bfloat16)

    return apply_rows


def head_attention(queries, query_ids, prefix_keys, prefix_values, suffix_kv, suffix_ids, score_scale):
    prefix_scores = (
        jnp.einsum("bqd,kd->bqk", queries, prefix_keys, preferred_element_type=jnp.float32)
        * score_scale
    )
    near_scores = (
        jnp.einsum("bqd,bkd->bqk", queries, suffix_kv[:, :, 0], preferred_element_type=jnp.float32)
        * score_scale
    )
    allowed = query_ids[:, :, None] == suffix_ids[:, None, :]
    near_scores = jnp.where(allowed, near_scores, -jnp.inf)
    row_top = jnp.maximum(jnp.max(prefix_scores, axis=-1), jnp.max(near_scores, axis=-1))
    prefix_weights = jnp.exp(prefix_scores - row_top[:, :, None])
    near_weights = jnp.exp(near_scores - row_top[:, :, None])
    row_total = jnp.sum(prefix_weights, axis=-1) + jnp.sum(near_weights, axis=-1)
    mixed = jnp.einsum(
        "bqk,kd->bqd",
        prefix_weights.astype(jnp.bfloat16),
        prefix_values,
        preferred_element_type=jnp.float32,
    ) + jnp.einsum(
        "bqk,bkd->bqd",
        near_weights.astype(jnp.bfloat16),
        suffix_kv[:, :, 1],
        preferred_element_type=jnp.float32,
    )
    return (mixed / row_total[:, :, None]).astype(jnp.bfloat16)


def on_device(
    inputs,
    request,
    prefix_cache,
    norm1_gain,
    w_qkv,
    w_out,
    norm2_gain,
    w_gate,
    w_up,
    w_down,
    norm3_gain,
    w_next,
):
    tokens = inputs[0]
    tok_rows, model_width = tokens.shape
    head_count = HEADS
    head_size = model_width // head_count
    score_scale = 1.0 / math.sqrt(head_size)
    class_size = lax.axis_size(CLASS)
    core = lax.axis_index("core")
    cache = prefix_cache[0]
    cache_rows = cache.shape[0]
    prefix_kv = cache.reshape(cache_rows, 2, head_count, head_size).transpose(2, 1, 0, 3)
    class_index = lax.axis_index(CLASS)
    rolled = jnp.take(
        prefix_kv, (class_index + jnp.arange(class_size, dtype=jnp.int32)) % class_size, axis=0
    )
    pieces = [rolled[0]] + [
        lax.ppermute(rolled[shift], CLASS, [(i, (i + shift) % class_size) for i in range(class_size)])
        for shift in range(1, class_size)
    ]
    class_prefix = jnp.stack(pieces)
    partner_prefix = lax.ppermute(class_prefix, "core", [(0, 1), (1, 0)])
    group_prefix = jnp.concatenate([class_prefix, partner_prefix], axis=0)
    prefix_keys = group_prefix[:, 0].reshape(-1, head_size)
    prefix_values = group_prefix[:, 1].reshape(-1, head_size)
    normed_in = rms_norm(tokens, norm1_gain)
    projected = return_rows(gather_rows(normed_in, projector(w_qkv)))
    own_qkv = projected.reshape(tok_rows, 3, head_count, head_size).transpose(2, 0, 1, 3)
    class_qkv = lax.all_to_all(own_qkv, CLASS, 0, 0, tiled=True)
    head_queries = class_qkv[:, :, 0]
    class_kv = class_qkv[:, :, 1:]
    partner_kv = lax.ppermute(class_kv, "core", [(0, 1), (1, 0)])
    pad_kv = jnp.zeros((1,) + partner_kv.shape[1:], partner_kv.dtype)
    padded_kv = jnp.concatenate([pad_kv, partner_kv, pad_kv], axis=0)
    before_kv = lax.dynamic_slice_in_dim(padded_kv, core, class_size, 0)
    after_kv = lax.dynamic_slice_in_dim(padded_kv, core + 1, class_size, 0)
    near_kv = jnp.concatenate([before_kv, class_kv, after_kv], axis=1)
    dev_ids = request[0].reshape(2 * class_size, tok_rows)
    pad_ids = jnp.full((1, tok_rows), -1, jnp.int32)
    padded_ids = jnp.concatenate([pad_ids, dev_ids, pad_ids], axis=0)
    window = lax.dynamic_slice_in_dim(padded_ids, core, 2 * class_size + 1, 0)
    query_ids = window[1::2]
    near_ids = jnp.concatenate([window[0:-1:2], query_ids, window[2::2]], axis=1)
    head_out = head_attention(
        head_queries, query_ids, prefix_keys, prefix_values, near_kv, near_ids, score_scale
    )
    back = lax.all_to_all(head_out, CLASS, 0, 0, tiled=True)
    attended = back.transpose(1, 0, 2).reshape(tok_rows, model_width)
    after_attn = (
        tokens.astype(jnp.float32) + jnp.dot(attended, w_out, preferred_element_type=jnp.float32)
    ).astype(jnp.bfloat16)

    def expand(portion, offset):
        normed_mid = rms_norm(portion, norm2_gain)
        gate_proj = jnp.dot(normed_mid, w_gate, preferred_element_type=jnp.float32)
        up_proj = jnp.dot(normed_mid, w_up, preferred_element_type=jnp.float32)
        return (jax.nn.silu(gate_proj) * up_proj).astype(jnp.bfloat16)

    hidden = gather_rows(after_attn, expand)
    own_sums = scatter_sums(jnp.dot(hidden, w_down, preferred_element_type=jnp.float32))
    layer_out = (after_attn.astype(jnp.float32) + own_sums).astype(jnp.bfloat16)
    next_qkv = return_rows(gather_rows(rms_norm(layer_out, norm3_gain), projector(w_next)))
    return (attended[None], layer_out[None], next_qkv[None])


def solution(mesh):
    group_count, dev_count = mesh.devices.shape
    fine = Mesh(
        mesh.devices.reshape(group_count, dev_count // 4, 2, 2), ("group", "z", "yh", "core")
    )
    in_specs = (
        P("group", DEV, None),
        P("group", None),
        P("group", DEV, None),
        P(),
        P(None, "group"),
        P(),
        P(),
        P(None, "group"),
        P(None, "group"),
        P("group", None),
        P(),
        P(None, "group"),
    )
    out_specs = (P("group", DEV, None), P("group", DEV, None), P("group", DEV, None))
    return jax.shard_map(
        on_device, mesh=fine, in_specs=in_specs, out_specs=out_specs, check_vma=False
    )
```

```python
import functools
import math

import jax
import jax.numpy as jnp
from jax import lax
from jax.experimental import pallas as pl
from jax.sharding import Mesh
from jax.sharding import PartitionSpec as P

HEADS = 16


NORM_EPSILON = 1e-05

CLASS = ("z", "yh")
DEV = ("z", "yh", "core")


def rms_norm(values, gain):
    wide = values.astype(jnp.float32)
    factor = lax.rsqrt(jnp.mean(wide * wide, axis=-1, keepdims=True) + NORM_EPSILON)
    return (wide * factor * gain).astype(jnp.bfloat16)


def gather_rows(values, handler):
    count = lax.axis_size("group")
    copies = jnp.broadcast_to(values[None], (count,) + values.shape)
    gathered = lax.all_to_all(copies, "group", 0, 0, tiled=True)
    return handler(gathered.reshape(-1, values.shape[-1]), jnp.int32(0))


def scatter_sums(partial):
    count = lax.axis_size("group")
    pieces = partial.reshape(count, -1, partial.shape[-1])
    return jnp.sum(lax.all_to_all(pieces, "group", 0, 0, tiled=True), axis=0)


def return_rows(columns):
    return lax.all_to_all(columns, "group", split_axis=0, concat_axis=1, tiled=True)


def projector(weight):

    def apply_rows(portion, offset):
        return jnp.dot(portion, weight, preferred_element_type=jnp.float32).astype(jnp.bfloat16)

    return apply_rows


def head_attention(queries, query_ids, prefix_keys, prefix_values, suffix_kv, suffix_ids, score_scale):
    prefix_scores = (
        jnp.einsum("bqd,kd->bqk", queries, prefix_keys, preferred_element_type=jnp.float32)
        * score_scale
    )
    near_scores = (
        jnp.einsum("bqd,bkd->bqk", queries, suffix_kv[:, :, 0], preferred_element_type=jnp.float32)
        * score_scale
    )
    allowed = query_ids[:, :, None] == suffix_ids[:, None, :]
    near_scores = jnp.where(allowed, near_scores, -jnp.inf)
    row_top = jnp.maximum(jnp.max(prefix_scores, axis=-1), jnp.max(near_scores, axis=-1))
    prefix_weights = jnp.exp(prefix_scores - row_top[:, :, None])
    near_weights = jnp.exp(near_scores - row_top[:, :, None])
    row_total = jnp.sum(prefix_weights, axis=-1) + jnp.sum(near_weights, axis=-1)
    mixed = jnp.einsum(
        "bqk,kd->bqd",
        prefix_weights.astype(jnp.bfloat16),
        prefix_values,
        preferred_element_type=jnp.float32,
    ) + jnp.einsum(
        "bqk,bkd->bqd",
        near_weights.astype(jnp.bfloat16),
        suffix_kv[:, :, 1],
        preferred_element_type=jnp.float32,
    )
    return (mixed / row_total[:, :, None]).astype(jnp.bfloat16)


def _attend_kernel(q_ref, pk_ref, pv_ref, nk_ref, nv_ref, bias_ref, o_ref, *, scale, sub):
    q = q_ref[...]
    dims = (((1,), (1,)), ((), ()))
    prefix_scores = lax.dot_general(q, pk_ref[...], dims, preferred_element_type=jnp.float32) * scale
    prefix_top = jnp.max(prefix_scores, axis=1, keepdims=True)
    for j in range(q.shape[0] // sub):
        rows = slice(j * sub, (j + 1) * sub)
        near_scores = (
            lax.dot_general(q[rows], nk_ref[j], dims, preferred_element_type=jnp.float32) * scale
            + bias_ref[j]
        )
        top = jnp.maximum(prefix_top[rows], jnp.max(near_scores, axis=1, keepdims=True))
        prefix_weights = jnp.exp(prefix_scores[rows] - top)
        near_weights = jnp.exp(near_scores - top)
        total = jnp.sum(prefix_weights, axis=1, keepdims=True) + jnp.sum(
            near_weights, axis=1, keepdims=True
        )
        mixed = jnp.dot(
            prefix_weights.astype(jnp.bfloat16), pv_ref[...], preferred_element_type=jnp.float32
        ) + jnp.dot(near_weights.astype(jnp.bfloat16), nv_ref[j], preferred_element_type=jnp.float32)
        o_ref[rows, :] = (mixed / total).astype(o_ref.dtype)


def attend(queries, prefix_keys, prefix_values, near_keys, near_values, bias, scale, block=128):
    rows, head_size = queries.shape
    sub = near_keys.shape[1] // 3
    per = block // sub
    keys_n = prefix_keys.shape[0]
    near_n = near_keys.shape[1]
    return pl.pallas_call(
        functools.partial(_attend_kernel, scale=scale, sub=sub),
        grid=(rows // block,),
        in_specs=[
            pl.BlockSpec((block, head_size), lambda i: (i, 0)),
            pl.BlockSpec((keys_n, head_size), lambda i: (0, 0)),
            pl.BlockSpec((keys_n, head_size), lambda i: (0, 0)),
            pl.BlockSpec((per, near_n, head_size), lambda i: (i, 0, 0)),
            pl.BlockSpec((per, near_n, head_size), lambda i: (i, 0, 0)),
            pl.BlockSpec((per, sub, near_n), lambda i: (i, 0, 0)),
        ],
        out_specs=pl.BlockSpec((block, head_size), lambda i: (i, 0)),
        out_shape=jax.ShapeDtypeStruct((rows, head_size), queries.dtype),
    )(queries, prefix_keys, prefix_values, near_keys, near_values, bias)


def on_device(
    inputs,
    request,
    prefix_cache,
    norm1_gain,
    w_qkv,
    w_out,
    norm2_gain,
    w_gate,
    w_up,
    w_down,
    norm3_gain,
    w_next,
):
    tokens = inputs[0]
    tok_rows, model_width = tokens.shape
    head_count = HEADS
    head_size = model_width // head_count
    score_scale = 1.0 / math.sqrt(head_size)
    class_size = lax.axis_size(CLASS)
    core = lax.axis_index("core")
    cache = prefix_cache[0]
    cache_rows = cache.shape[0]
    prefix_kv = cache.reshape(cache_rows, 2, head_count, head_size).transpose(2, 1, 0, 3)
    class_index = lax.axis_index(CLASS)
    rolled = jnp.take(
        prefix_kv, (class_index + jnp.arange(class_size, dtype=jnp.int32)) % class_size, axis=0
    )
    pieces = [rolled[0]] + [
        lax.ppermute(rolled[shift], CLASS, [(i, (i + shift) % class_size) for i in range(class_size)])
        for shift in range(1, class_size)
    ]
    class_prefix = jnp.stack(pieces)
    partner_prefix = lax.ppermute(class_prefix, "core", [(0, 1), (1, 0)])
    group_prefix = jnp.concatenate([class_prefix, partner_prefix], axis=0)
    prefix_keys = group_prefix[:, 0].reshape(-1, head_size)
    prefix_values = group_prefix[:, 1].reshape(-1, head_size)
    normed_in = rms_norm(tokens, norm1_gain)
    projected = return_rows(gather_rows(normed_in, projector(w_qkv)))
    own_qkv = projected.reshape(tok_rows, 3, head_count, head_size).transpose(2, 0, 1, 3)
    class_qkv = lax.all_to_all(own_qkv, CLASS, 0, 0, tiled=True)
    head_queries = class_qkv[:, :, 0]
    class_kv = class_qkv[:, :, 1:]
    partner_kv = lax.ppermute(class_kv, "core", [(0, 1), (1, 0)])
    pad_kv = jnp.zeros((1,) + partner_kv.shape[1:], partner_kv.dtype)
    padded_kv = jnp.concatenate([pad_kv, partner_kv, pad_kv], axis=0)
    before_kv = lax.dynamic_slice_in_dim(padded_kv, core, class_size, 0)
    after_kv = lax.dynamic_slice_in_dim(padded_kv, core + 1, class_size, 0)
    near_kv = jnp.concatenate([before_kv, class_kv, after_kv], axis=1)
    dev_ids = request[0].reshape(2 * class_size, tok_rows)
    pad_ids = jnp.full((1, tok_rows), -1, jnp.int32)
    padded_ids = jnp.concatenate([pad_ids, dev_ids, pad_ids], axis=0)
    window = lax.dynamic_slice_in_dim(padded_ids, core, 2 * class_size + 1, 0)
    query_ids = window[1::2]
    near_ids = jnp.concatenate([window[0:-1:2], query_ids, window[2::2]], axis=1)
    bias = jnp.where(query_ids[:, :, None] == near_ids[:, None, :], 0.0, -jnp.inf)
    head_out = attend(
        head_queries.reshape(-1, head_size),
        prefix_keys,
        prefix_values,
        near_kv[:, :, 0],
        near_kv[:, :, 1],
        bias.astype(jnp.float32),
        score_scale,
    ).reshape(class_size, tok_rows, head_size)
    back = lax.all_to_all(head_out, CLASS, 0, 0, tiled=True)
    attended = back.transpose(1, 0, 2).reshape(tok_rows, model_width)
    after_attn = (
        tokens.astype(jnp.float32) + jnp.dot(attended, w_out, preferred_element_type=jnp.float32)
    ).astype(jnp.bfloat16)

    def expand(portion, offset):
        normed_mid = rms_norm(portion, norm2_gain)
        gate_proj = jnp.dot(normed_mid, w_gate, preferred_element_type=jnp.float32)
        up_proj = jnp.dot(normed_mid, w_up, preferred_element_type=jnp.float32)
        return (jax.nn.silu(gate_proj) * up_proj).astype(jnp.bfloat16)

    hidden = gather_rows(after_attn, expand)
    own_sums = scatter_sums(jnp.dot(hidden, w_down, preferred_element_type=jnp.float32))
    layer_out = (after_attn.astype(jnp.float32) + own_sums).astype(jnp.bfloat16)
    next_qkv = return_rows(gather_rows(rms_norm(layer_out, norm3_gain), projector(w_next)))
    return (attended[None], layer_out[None], next_qkv[None])


def solution(mesh):
    group_count, dev_count = mesh.devices.shape
    fine = Mesh(
        mesh.devices.reshape(group_count, dev_count // 4, 2, 2), ("group", "z", "yh", "core")
    )
    in_specs = (
        P("group", DEV, None),
        P("group", None),
        P("group", DEV, None),
        P(),
        P(None, "group"),
        P(),
        P(),
        P(None, "group"),
        P(None, "group"),
        P("group", None),
        P(),
        P(None, "group"),
    )
    out_specs = (P("group", DEV, None), P("group", DEV, None), P("group", DEV, None))
    return jax.shard_map(
        on_device, mesh=fine, in_specs=in_specs, out_specs=out_specs, check_vma=False
    )
```

```python
import functools
import math

import jax
import jax.numpy as jnp
from jax import lax
from jax.experimental import pallas as pl
from jax.sharding import Mesh
from jax.sharding import PartitionSpec as P

HEADS = 16


NORM_EPSILON = 1e-05

CLASS = ("z", "yh")
DEV = ("z", "yh", "core")


def rms_norm(values, gain):
    wide = values.astype(jnp.float32)
    factor = lax.rsqrt(jnp.mean(wide * wide, axis=-1, keepdims=True) + NORM_EPSILON)
    return (wide * factor * gain).astype(jnp.bfloat16)


def gather_rows(values, handler):
    count = lax.axis_size("group")
    copies = jnp.broadcast_to(values[None], (count,) + values.shape)
    gathered = lax.all_to_all(copies, "group", 0, 0, tiled=True)
    return handler(gathered.reshape(-1, values.shape[-1]), jnp.int32(0))


def scatter_sums(partial):
    count = lax.axis_size("group")
    pieces = partial.reshape(count, -1, partial.shape[-1])
    return jnp.sum(lax.all_to_all(pieces, "group", 0, 0, tiled=True), axis=0)


def return_rows(columns):
    return lax.all_to_all(columns, "group", split_axis=0, concat_axis=1, tiled=True)


def projector(weight):

    def apply_rows(portion, offset):
        return jnp.dot(portion, weight, preferred_element_type=jnp.float32).astype(jnp.bfloat16)

    return apply_rows


def head_attention(queries, query_ids, prefix_keys, prefix_values, suffix_kv, suffix_ids, score_scale):
    prefix_scores = (
        jnp.einsum("bqd,kd->bqk", queries, prefix_keys, preferred_element_type=jnp.float32)
        * score_scale
    )
    near_scores = (
        jnp.einsum("bqd,bkd->bqk", queries, suffix_kv[:, :, 0], preferred_element_type=jnp.float32)
        * score_scale
    )
    allowed = query_ids[:, :, None] == suffix_ids[:, None, :]
    near_scores = jnp.where(allowed, near_scores, -jnp.inf)
    row_top = jnp.maximum(jnp.max(prefix_scores, axis=-1), jnp.max(near_scores, axis=-1))
    prefix_weights = jnp.exp(prefix_scores - row_top[:, :, None])
    near_weights = jnp.exp(near_scores - row_top[:, :, None])
    row_total = jnp.sum(prefix_weights, axis=-1) + jnp.sum(near_weights, axis=-1)
    mixed = jnp.einsum(
        "bqk,kd->bqd",
        prefix_weights.astype(jnp.bfloat16),
        prefix_values,
        preferred_element_type=jnp.float32,
    ) + jnp.einsum(
        "bqk,bkd->bqd",
        near_weights.astype(jnp.bfloat16),
        suffix_kv[:, :, 1],
        preferred_element_type=jnp.float32,
    )
    return (mixed / row_total[:, :, None]).astype(jnp.bfloat16)


def _attend_kernel(q_ref, pk_ref, pv_ref, nk_ref, nv_ref, bias_ref, o_ref, *, scale, sub):
    q = q_ref[...]
    dims = (((1,), (1,)), ((), ()))
    prefix_scores = jnp.dot(q, pk_ref[...], preferred_element_type=jnp.float32) * scale
    prefix_top = jnp.max(prefix_scores, axis=1, keepdims=True)
    for j in range(q.shape[0] // sub):
        rows = slice(j * sub, (j + 1) * sub)
        near_scores = (
            lax.dot_general(q[rows], nk_ref[j], dims, preferred_element_type=jnp.float32) * scale
            + bias_ref[j]
        )
        top = jnp.maximum(prefix_top[rows], jnp.max(near_scores, axis=1, keepdims=True))
        prefix_weights = jnp.exp(prefix_scores[rows] - top)
        near_weights = jnp.exp(near_scores - top)
        total = jnp.sum(prefix_weights, axis=1, keepdims=True) + jnp.sum(
            near_weights, axis=1, keepdims=True
        )
        mixed = jnp.dot(
            prefix_weights.astype(jnp.bfloat16), pv_ref[...], preferred_element_type=jnp.float32
        ) + jnp.dot(near_weights.astype(jnp.bfloat16), nv_ref[j], preferred_element_type=jnp.float32)
        o_ref[rows, :] = (mixed / total).astype(o_ref.dtype)


def attend(queries, prefix_keys_t, prefix_values, near_keys, near_values, bias, scale, block=256):
    rows, head_size = queries.shape
    sub = near_keys.shape[1] // 3
    per = block // sub
    keys_n = prefix_values.shape[0]
    near_n = near_keys.shape[1]
    return pl.pallas_call(
        functools.partial(_attend_kernel, scale=scale, sub=sub),
        grid=(rows // block,),
        in_specs=[
            pl.BlockSpec((block, head_size), lambda i: (i, 0)),
            pl.BlockSpec((head_size, keys_n), lambda i: (0, 0)),
            pl.BlockSpec((keys_n, head_size), lambda i: (0, 0)),
            pl.BlockSpec((per, near_n, head_size), lambda i: (i, 0, 0)),
            pl.BlockSpec((per, near_n, head_size), lambda i: (i, 0, 0)),
            pl.BlockSpec((per, sub, near_n), lambda i: (i, 0, 0)),
        ],
        out_specs=pl.BlockSpec((block, head_size), lambda i: (i, 0)),
        out_shape=jax.ShapeDtypeStruct((rows, head_size), queries.dtype),
    )(queries, prefix_keys_t, prefix_values, near_keys, near_values, bias)


def on_device(
    inputs,
    request,
    prefix_cache,
    norm1_gain,
    w_qkv,
    w_out,
    norm2_gain,
    w_gate,
    w_up,
    w_down,
    norm3_gain,
    w_next,
):
    tokens = inputs[0]
    tok_rows, model_width = tokens.shape
    head_count = HEADS
    head_size = model_width // head_count
    score_scale = 1.0 / math.sqrt(head_size)
    class_size = lax.axis_size(CLASS)
    core = lax.axis_index("core")
    cache = prefix_cache[0]
    cache_rows = cache.shape[0]
    prefix_kv = cache.reshape(cache_rows, 2, head_count, head_size).transpose(2, 1, 0, 3)
    class_index = lax.axis_index(CLASS)
    rolled = jnp.take(
        prefix_kv, (class_index + jnp.arange(class_size, dtype=jnp.int32)) % class_size, axis=0
    )
    pieces = [rolled[0]] + [
        lax.ppermute(rolled[shift], CLASS, [(i, (i + shift) % class_size) for i in range(class_size)])
        for shift in range(1, class_size)
    ]
    class_prefix = jnp.stack(pieces)
    partner_prefix = lax.ppermute(class_prefix, "core", [(0, 1), (1, 0)])
    group_prefix = jnp.concatenate([class_prefix, partner_prefix], axis=0)
    prefix_keys = group_prefix[:, 0].reshape(-1, head_size)
    prefix_values = group_prefix[:, 1].reshape(-1, head_size)
    normed_in = rms_norm(tokens, norm1_gain)
    projected = return_rows(gather_rows(normed_in, projector(w_qkv)))
    own_qkv = projected.reshape(tok_rows, 3, head_count, head_size).transpose(2, 0, 1, 3)
    class_qkv = lax.all_to_all(own_qkv, CLASS, 0, 0, tiled=True)
    head_queries = class_qkv[:, :, 0]
    class_kv = class_qkv[:, :, 1:]
    partner_kv = lax.ppermute(class_kv, "core", [(0, 1), (1, 0)])
    pad_kv = jnp.zeros((1,) + partner_kv.shape[1:], partner_kv.dtype)
    padded_kv = jnp.concatenate([pad_kv, partner_kv, pad_kv], axis=0)
    before_kv = lax.dynamic_slice_in_dim(padded_kv, core, class_size, 0)
    after_kv = lax.dynamic_slice_in_dim(padded_kv, core + 1, class_size, 0)
    near_kv = jnp.concatenate([before_kv, class_kv, after_kv], axis=1)
    dev_ids = request[0].reshape(2 * class_size, tok_rows)
    pad_ids = jnp.full((1, tok_rows), -1, jnp.int32)
    padded_ids = jnp.concatenate([pad_ids, dev_ids, pad_ids], axis=0)
    window = lax.dynamic_slice_in_dim(padded_ids, core, 2 * class_size + 1, 0)
    query_ids = window[1::2]
    near_ids = jnp.concatenate([window[0:-1:2], query_ids, window[2::2]], axis=1)
    bias = jnp.where(query_ids[:, :, None] == near_ids[:, None, :], 0.0, -jnp.inf)
    head_out = attend(
        head_queries.reshape(-1, head_size),
        prefix_keys.T,
        prefix_values,
        near_kv[:, :, 0],
        near_kv[:, :, 1],
        bias.astype(jnp.float32),
        score_scale,
    ).reshape(class_size, tok_rows, head_size)
    back = lax.all_to_all(head_out, CLASS, 0, 0, tiled=True)
    attended = back.transpose(1, 0, 2).reshape(tok_rows, model_width)
    after_attn = (
        tokens.astype(jnp.float32) + jnp.dot(attended, w_out, preferred_element_type=jnp.float32)
    ).astype(jnp.bfloat16)

    def expand(portion, offset):
        normed_mid = rms_norm(portion, norm2_gain)
        gate_proj = jnp.dot(normed_mid, w_gate, preferred_element_type=jnp.float32)
        up_proj = jnp.dot(normed_mid, w_up, preferred_element_type=jnp.float32)
        return (jax.nn.silu(gate_proj) * up_proj).astype(jnp.bfloat16)

    hidden = gather_rows(after_attn, expand)
    own_sums = scatter_sums(jnp.dot(hidden, w_down, preferred_element_type=jnp.float32))
    layer_out = (after_attn.astype(jnp.float32) + own_sums).astype(jnp.bfloat16)
    next_qkv = return_rows(gather_rows(rms_norm(layer_out, norm3_gain), projector(w_next)))
    return (attended[None], layer_out[None], next_qkv[None])


def solution(mesh):
    group_count, dev_count = mesh.devices.shape
    fine = Mesh(
        mesh.devices.reshape(group_count, dev_count // 4, 2, 2), ("group", "z", "yh", "core")
    )
    in_specs = (
        P("group", DEV, None),
        P("group", None),
        P("group", DEV, None),
        P(),
        P(None, "group"),
        P(),
        P(),
        P(None, "group"),
        P(None, "group"),
        P("group", None),
        P(),
        P(None, "group"),
    )
    out_specs = (P("group", DEV, None), P("group", DEV, None), P("group", DEV, None))
    return jax.shard_map(
        on_device, mesh=fine, in_specs=in_specs, out_specs=out_specs, check_vma=False
    )
```

```python
import functools
import math

import jax
import jax.numpy as jnp
from jax import lax
from jax.experimental import pallas as pl
from jax.sharding import Mesh
from jax.sharding import PartitionSpec as P

HEADS = 16


NORM_EPSILON = 1e-05

CLASS = ("z", "yh")
DEV = ("z", "yh", "core")


def rms_norm(values, gain):
    wide = values.astype(jnp.float32)
    factor = lax.rsqrt(jnp.mean(wide * wide, axis=-1, keepdims=True) + NORM_EPSILON)
    return (wide * factor * gain).astype(jnp.bfloat16)


def gather_rows(values, handler):
    count = lax.axis_size("group")
    copies = jnp.broadcast_to(values[None], (count,) + values.shape)
    gathered = lax.all_to_all(copies, "group", 0, 0, tiled=True)
    return handler(gathered.reshape(-1, values.shape[-1]), jnp.int32(0))


def scatter_sums(partial):
    count = lax.axis_size("group")
    pieces = partial.reshape(count, -1, partial.shape[-1])
    sent = lax.all_to_all(pieces.astype(jnp.bfloat16), "group", 0, 0, tiled=True)
    return jnp.sum(sent.astype(jnp.float32), axis=0)


def return_rows(columns):
    return lax.all_to_all(columns, "group", split_axis=0, concat_axis=1, tiled=True)


def projector(weight):

    def apply_rows(portion, offset):
        return jnp.dot(portion, weight, preferred_element_type=jnp.float32).astype(jnp.bfloat16)

    return apply_rows


def head_attention(queries, query_ids, prefix_keys, prefix_values, suffix_kv, suffix_ids, score_scale):
    prefix_scores = (
        jnp.einsum("bqd,kd->bqk", queries, prefix_keys, preferred_element_type=jnp.float32)
        * score_scale
    )
    near_scores = (
        jnp.einsum("bqd,bkd->bqk", queries, suffix_kv[:, :, 0], preferred_element_type=jnp.float32)
        * score_scale
    )
    allowed = query_ids[:, :, None] == suffix_ids[:, None, :]
    near_scores = jnp.where(allowed, near_scores, -jnp.inf)
    row_top = jnp.maximum(jnp.max(prefix_scores, axis=-1), jnp.max(near_scores, axis=-1))
    prefix_weights = jnp.exp(prefix_scores - row_top[:, :, None])
    near_weights = jnp.exp(near_scores - row_top[:, :, None])
    row_total = jnp.sum(prefix_weights, axis=-1) + jnp.sum(near_weights, axis=-1)
    mixed = jnp.einsum(
        "bqk,kd->bqd",
        prefix_weights.astype(jnp.bfloat16),
        prefix_values,
        preferred_element_type=jnp.float32,
    ) + jnp.einsum(
        "bqk,bkd->bqd",
        near_weights.astype(jnp.bfloat16),
        suffix_kv[:, :, 1],
        preferred_element_type=jnp.float32,
    )
    return (mixed / row_total[:, :, None]).astype(jnp.bfloat16)


def _attend_kernel(q_ref, pk_ref, pv_ref, nk_ref, nv_ref, bias_ref, o_ref, *, scale, sub):
    q = q_ref[...]
    dims = (((1,), (1,)), ((), ()))
    prefix_scores = jnp.dot(q, pk_ref[...], preferred_element_type=jnp.float32) * scale
    prefix_top = jnp.max(prefix_scores, axis=1, keepdims=True)
    for j in range(q.shape[0] // sub):
        rows = slice(j * sub, (j + 1) * sub)
        near_scores = (
            lax.dot_general(q[rows], nk_ref[j], dims, preferred_element_type=jnp.float32) * scale
            + bias_ref[j]
        )
        top = jnp.maximum(prefix_top[rows], jnp.max(near_scores, axis=1, keepdims=True))
        prefix_weights = jnp.exp(prefix_scores[rows] - top)
        near_weights = jnp.exp(near_scores - top)
        total = jnp.sum(prefix_weights, axis=1, keepdims=True) + jnp.sum(
            near_weights, axis=1, keepdims=True
        )
        mixed = jnp.dot(
            prefix_weights.astype(jnp.bfloat16), pv_ref[...], preferred_element_type=jnp.float32
        ) + jnp.dot(near_weights.astype(jnp.bfloat16), nv_ref[j], preferred_element_type=jnp.float32)
        o_ref[rows, :] = (mixed / total).astype(o_ref.dtype)


def attend(queries, prefix_keys_t, prefix_values, near_keys, near_values, bias, scale, block=256):
    rows, head_size = queries.shape
    sub = near_keys.shape[1] // 3
    per = block // sub
    keys_n = prefix_values.shape[0]
    near_n = near_keys.shape[1]
    return pl.pallas_call(
        functools.partial(_attend_kernel, scale=scale, sub=sub),
        grid=(rows // block,),
        in_specs=[
            pl.BlockSpec((block, head_size), lambda i: (i, 0)),
            pl.BlockSpec((head_size, keys_n), lambda i: (0, 0)),
            pl.BlockSpec((keys_n, head_size), lambda i: (0, 0)),
            pl.BlockSpec((per, near_n, head_size), lambda i: (i, 0, 0)),
            pl.BlockSpec((per, near_n, head_size), lambda i: (i, 0, 0)),
            pl.BlockSpec((per, sub, near_n), lambda i: (i, 0, 0)),
        ],
        out_specs=pl.BlockSpec((block, head_size), lambda i: (i, 0)),
        out_shape=jax.ShapeDtypeStruct((rows, head_size), queries.dtype),
    )(queries, prefix_keys_t, prefix_values, near_keys, near_values, bias)


def on_device(
    inputs,
    request,
    prefix_cache,
    norm1_gain,
    w_qkv,
    w_out,
    norm2_gain,
    w_gate,
    w_up,
    w_down,
    norm3_gain,
    w_next,
):
    tokens = inputs[0]
    tok_rows, model_width = tokens.shape
    head_count = HEADS
    head_size = model_width // head_count
    score_scale = 1.0 / math.sqrt(head_size)
    class_size = lax.axis_size(CLASS)
    core = lax.axis_index("core")
    cache = prefix_cache[0]
    cache_rows = cache.shape[0]
    prefix_kv = cache.reshape(cache_rows, 2, head_count, head_size).transpose(2, 1, 0, 3)
    class_index = lax.axis_index(CLASS)
    rolled = jnp.take(
        prefix_kv, (class_index + jnp.arange(class_size, dtype=jnp.int32)) % class_size, axis=0
    )
    pieces = [rolled[0]] + [
        lax.ppermute(rolled[shift], CLASS, [(i, (i + shift) % class_size) for i in range(class_size)])
        for shift in range(1, class_size)
    ]
    class_prefix = jnp.stack(pieces)
    partner_prefix = lax.ppermute(class_prefix, "core", [(0, 1), (1, 0)])
    group_prefix = jnp.concatenate([class_prefix, partner_prefix], axis=0)
    prefix_keys = group_prefix[:, 0].reshape(-1, head_size)
    prefix_values = group_prefix[:, 1].reshape(-1, head_size)
    normed_in = rms_norm(tokens, norm1_gain)
    projected = return_rows(gather_rows(normed_in, projector(w_qkv)))
    own_qkv = projected.reshape(tok_rows, 3, head_count, head_size).transpose(2, 0, 1, 3)
    class_qkv = lax.all_to_all(own_qkv, CLASS, 0, 0, tiled=True)
    head_queries = class_qkv[:, :, 0]
    class_kv = class_qkv[:, :, 1:]
    partner_kv = lax.ppermute(class_kv, "core", [(0, 1), (1, 0)])
    pad_kv = jnp.zeros((1,) + partner_kv.shape[1:], partner_kv.dtype)
    padded_kv = jnp.concatenate([pad_kv, partner_kv, pad_kv], axis=0)
    before_kv = lax.dynamic_slice_in_dim(padded_kv, core, class_size, 0)
    after_kv = lax.dynamic_slice_in_dim(padded_kv, core + 1, class_size, 0)
    near_kv = jnp.concatenate([before_kv, class_kv, after_kv], axis=1)
    dev_ids = request[0].reshape(2 * class_size, tok_rows)
    pad_ids = jnp.full((1, tok_rows), -1, jnp.int32)
    padded_ids = jnp.concatenate([pad_ids, dev_ids, pad_ids], axis=0)
    window = lax.dynamic_slice_in_dim(padded_ids, core, 2 * class_size + 1, 0)
    query_ids = window[1::2]
    near_ids = jnp.concatenate([window[0:-1:2], query_ids, window[2::2]], axis=1)
    bias = jnp.where(query_ids[:, :, None] == near_ids[:, None, :], 0.0, -jnp.inf)
    head_out = attend(
        head_queries.reshape(-1, head_size),
        prefix_keys.T,
        prefix_values,
        near_kv[:, :, 0],
        near_kv[:, :, 1],
        bias.astype(jnp.float32),
        score_scale,
    ).reshape(class_size, tok_rows, head_size)
    back = lax.all_to_all(head_out, CLASS, 0, 0, tiled=True)
    attended = back.transpose(1, 0, 2).reshape(tok_rows, model_width)
    after_attn = (
        tokens.astype(jnp.float32) + jnp.dot(attended, w_out, preferred_element_type=jnp.float32)
    ).astype(jnp.bfloat16)

    def expand(portion, offset):
        normed_mid = rms_norm(portion, norm2_gain)
        gate_proj = jnp.dot(normed_mid, w_gate, preferred_element_type=jnp.float32)
        up_proj = jnp.dot(normed_mid, w_up, preferred_element_type=jnp.float32)
        return (jax.nn.silu(gate_proj) * up_proj).astype(jnp.bfloat16)

    hidden = gather_rows(after_attn, expand)
    own_sums = scatter_sums(jnp.dot(hidden, w_down, preferred_element_type=jnp.float32))
    layer_out = (after_attn.astype(jnp.float32) + own_sums).astype(jnp.bfloat16)
    next_qkv = return_rows(gather_rows(rms_norm(layer_out, norm3_gain), projector(w_next)))
    return (attended[None], layer_out[None], next_qkv[None])


def solution(mesh):
    group_count, dev_count = mesh.devices.shape
    fine = Mesh(
        mesh.devices.reshape(group_count, dev_count // 4, 2, 2), ("group", "z", "yh", "core")
    )
    in_specs = (
        P("group", DEV, None),
        P("group", None),
        P("group", DEV, None),
        P(),
        P(None, "group"),
        P(),
        P(),
        P(None, "group"),
        P(None, "group"),
        P("group", None),
        P(),
        P(None, "group"),
    )
    out_specs = (P("group", DEV, None), P("group", DEV, None), P("group", DEV, None))
    return jax.shard_map(
        on_device, mesh=fine, in_specs=in_specs, out_specs=out_specs, check_vma=False
    )
```

```python
import functools
import math

import jax
import jax.numpy as jnp
from jax import lax
from jax.experimental import pallas as pl
from jax.sharding import Mesh
from jax.sharding import PartitionSpec as P

HEADS = 16


NORM_EPSILON = 1e-05

CLASS = ("z", "yh")
DEV = ("z", "yh", "core")


def rms_norm(values, gain):
    wide = values.astype(jnp.float32)
    factor = lax.rsqrt(jnp.mean(wide * wide, axis=-1, keepdims=True) + NORM_EPSILON)
    return (wide * factor * gain).astype(jnp.bfloat16)


def gather_rows(values, handler, by_permutes=False):
    count = lax.axis_size("group")
    if by_permutes:
        pieces = [values] + [
            lax.ppermute(values, "group", [(i, (i + shift) % count) for i in range(count)])
            for shift in range(1, count)
        ]
        own = lax.axis_index("group")
        order = (own - jnp.arange(count, dtype=jnp.int32)) % count
        gathered = jnp.take(jnp.stack(pieces), order, axis=0)
    else:
        copies = jnp.broadcast_to(values[None], (count,) + values.shape)
        gathered = lax.all_to_all(copies, "group", 0, 0, tiled=True)
    return handler(gathered.reshape(-1, values.shape[-1]), jnp.int32(0))


def scatter_sums(partial):
    count = lax.axis_size("group")
    pieces = partial.reshape(count, -1, partial.shape[-1])
    sent = lax.all_to_all(pieces.astype(jnp.bfloat16), "group", 0, 0, tiled=True)
    return jnp.sum(sent.astype(jnp.float32), axis=0)


def return_rows(columns):
    return lax.all_to_all(columns, "group", split_axis=0, concat_axis=1, tiled=True)


def projector(weight):

    def apply_rows(portion, offset):
        return jnp.dot(portion, weight, preferred_element_type=jnp.float32).astype(jnp.bfloat16)

    return apply_rows


def head_attention(queries, query_ids, prefix_keys, prefix_values, suffix_kv, suffix_ids, score_scale):
    prefix_scores = (
        jnp.einsum("bqd,kd->bqk", queries, prefix_keys, preferred_element_type=jnp.float32)
        * score_scale
    )
    near_scores = (
        jnp.einsum("bqd,bkd->bqk", queries, suffix_kv[:, :, 0], preferred_element_type=jnp.float32)
        * score_scale
    )
    allowed = query_ids[:, :, None] == suffix_ids[:, None, :]
    near_scores = jnp.where(allowed, near_scores, -jnp.inf)
    row_top = jnp.maximum(jnp.max(prefix_scores, axis=-1), jnp.max(near_scores, axis=-1))
    prefix_weights = jnp.exp(prefix_scores - row_top[:, :, None])
    near_weights = jnp.exp(near_scores - row_top[:, :, None])
    row_total = jnp.sum(prefix_weights, axis=-1) + jnp.sum(near_weights, axis=-1)
    mixed = jnp.einsum(
        "bqk,kd->bqd",
        prefix_weights.astype(jnp.bfloat16),
        prefix_values,
        preferred_element_type=jnp.float32,
    ) + jnp.einsum(
        "bqk,bkd->bqd",
        near_weights.astype(jnp.bfloat16),
        suffix_kv[:, :, 1],
        preferred_element_type=jnp.float32,
    )
    return (mixed / row_total[:, :, None]).astype(jnp.bfloat16)


def _attend_kernel(q_ref, pk_ref, pv_ref, nk_ref, nv_ref, bias_ref, o_ref, *, scale, sub):
    q = q_ref[...]
    dims = (((1,), (1,)), ((), ()))
    prefix_scores = jnp.dot(q, pk_ref[...], preferred_element_type=jnp.float32) * scale
    prefix_top = jnp.max(prefix_scores, axis=1, keepdims=True)
    for j in range(q.shape[0] // sub):
        rows = slice(j * sub, (j + 1) * sub)
        near_scores = (
            lax.dot_general(q[rows], nk_ref[j], dims, preferred_element_type=jnp.float32) * scale
            + bias_ref[j]
        )
        top = jnp.maximum(prefix_top[rows], jnp.max(near_scores, axis=1, keepdims=True))
        prefix_weights = jnp.exp(prefix_scores[rows] - top)
        near_weights = jnp.exp(near_scores - top)
        total = jnp.sum(prefix_weights, axis=1, keepdims=True) + jnp.sum(
            near_weights, axis=1, keepdims=True
        )
        mixed = jnp.dot(
            prefix_weights.astype(jnp.bfloat16), pv_ref[...], preferred_element_type=jnp.float32
        ) + jnp.dot(near_weights.astype(jnp.bfloat16), nv_ref[j], preferred_element_type=jnp.float32)
        o_ref[rows, :] = (mixed / total).astype(o_ref.dtype)


def attend(queries, prefix_keys_t, prefix_values, near_keys, near_values, bias, scale, block=256):
    rows, head_size = queries.shape
    sub = near_keys.shape[1] // 3
    per = block // sub
    keys_n = prefix_values.shape[0]
    near_n = near_keys.shape[1]
    return pl.pallas_call(
        functools.partial(_attend_kernel, scale=scale, sub=sub),
        grid=(rows // block,),
        in_specs=[
            pl.BlockSpec((block, head_size), lambda i: (i, 0)),
            pl.BlockSpec((head_size, keys_n), lambda i: (0, 0)),
            pl.BlockSpec((keys_n, head_size), lambda i: (0, 0)),
            pl.BlockSpec((per, near_n, head_size), lambda i: (i, 0, 0)),
            pl.BlockSpec((per, near_n, head_size), lambda i: (i, 0, 0)),
            pl.BlockSpec((per, sub, near_n), lambda i: (i, 0, 0)),
        ],
        out_specs=pl.BlockSpec((block, head_size), lambda i: (i, 0)),
        out_shape=jax.ShapeDtypeStruct((rows, head_size), queries.dtype),
    )(queries, prefix_keys_t, prefix_values, near_keys, near_values, bias)


def on_device(
    inputs,
    request,
    prefix_cache,
    norm1_gain,
    w_qkv,
    w_out,
    norm2_gain,
    w_gate,
    w_up,
    w_down,
    norm3_gain,
    w_next,
):
    tokens = inputs[0]
    tok_rows, model_width = tokens.shape
    head_count = HEADS
    head_size = model_width // head_count
    score_scale = 1.0 / math.sqrt(head_size)
    class_size = lax.axis_size(CLASS)
    core = lax.axis_index("core")
    cache = prefix_cache[0]
    cache_rows = cache.shape[0]
    prefix_kv = cache.reshape(cache_rows, 2, head_count, head_size).transpose(2, 1, 0, 3)
    class_prefix = lax.all_to_all(prefix_kv, CLASS, 0, 0, tiled=True)
    partner_prefix = lax.ppermute(class_prefix, "core", [(0, 1), (1, 0)])
    group_prefix = jnp.concatenate([class_prefix, partner_prefix], axis=0)
    prefix_keys = group_prefix[:, 0].reshape(-1, head_size)
    prefix_values = group_prefix[:, 1].reshape(-1, head_size)
    normed_in = rms_norm(tokens, norm1_gain)
    projected = return_rows(gather_rows(normed_in, projector(w_qkv), by_permutes=True))
    own_qkv = projected.reshape(tok_rows, 3, head_count, head_size).transpose(2, 0, 1, 3)
    class_qkv = lax.all_to_all(own_qkv, CLASS, 0, 0, tiled=True)
    head_queries = class_qkv[:, :, 0]
    class_kv = class_qkv[:, :, 1:]
    partner_kv = lax.ppermute(class_kv, "core", [(0, 1), (1, 0)])
    pad_kv = jnp.zeros((1,) + partner_kv.shape[1:], partner_kv.dtype)
    padded_kv = jnp.concatenate([pad_kv, partner_kv, pad_kv], axis=0)
    before_kv = lax.dynamic_slice_in_dim(padded_kv, core, class_size, 0)
    after_kv = lax.dynamic_slice_in_dim(padded_kv, core + 1, class_size, 0)
    near_kv = jnp.concatenate([before_kv, class_kv, after_kv], axis=1)
    dev_ids = request[0].reshape(2 * class_size, tok_rows)
    pad_ids = jnp.full((1, tok_rows), -1, jnp.int32)
    padded_ids = jnp.concatenate([pad_ids, dev_ids, pad_ids], axis=0)
    window = lax.dynamic_slice_in_dim(padded_ids, core, 2 * class_size + 1, 0)
    query_ids = window[1::2]
    near_ids = jnp.concatenate([window[0:-1:2], query_ids, window[2::2]], axis=1)
    bias = jnp.where(query_ids[:, :, None] == near_ids[:, None, :], 0.0, -jnp.inf)
    head_out = attend(
        head_queries.reshape(-1, head_size),
        prefix_keys.T,
        prefix_values,
        near_kv[:, :, 0],
        near_kv[:, :, 1],
        bias.astype(jnp.float32),
        score_scale,
    ).reshape(class_size, tok_rows, head_size)
    back = lax.all_to_all(head_out, CLASS, 0, 0, tiled=True)
    attended = back.transpose(1, 0, 2).reshape(tok_rows, model_width)
    after_attn = (
        tokens.astype(jnp.float32) + jnp.dot(attended, w_out, preferred_element_type=jnp.float32)
    ).astype(jnp.bfloat16)

    def expand(portion, offset):
        normed_mid = rms_norm(portion, norm2_gain)
        gate_proj = jnp.dot(normed_mid, w_gate, preferred_element_type=jnp.float32)
        up_proj = jnp.dot(normed_mid, w_up, preferred_element_type=jnp.float32)
        return (jax.nn.silu(gate_proj) * up_proj).astype(jnp.bfloat16)

    hidden = gather_rows(after_attn, expand)
    own_sums = scatter_sums(jnp.dot(hidden, w_down, preferred_element_type=jnp.float32))
    layer_out = (after_attn.astype(jnp.float32) + own_sums).astype(jnp.bfloat16)
    next_qkv = return_rows(gather_rows(rms_norm(layer_out, norm3_gain), projector(w_next)))
    return (attended[None], layer_out[None], next_qkv[None])


def solution(mesh):
    group_count, dev_count = mesh.devices.shape
    fine = Mesh(
        mesh.devices.reshape(group_count, dev_count // 4, 2, 2), ("group", "z", "yh", "core")
    )
    in_specs = (
        P("group", DEV, None),
        P("group", None),
        P("group", DEV, None),
        P(),
        P(None, "group"),
        P(),
        P(),
        P(None, "group"),
        P(None, "group"),
        P("group", None),
        P(),
        P(None, "group"),
    )
    out_specs = (P("group", DEV, None), P("group", DEV, None), P("group", DEV, None))
    return jax.shard_map(
        on_device, mesh=fine, in_specs=in_specs, out_specs=out_specs, check_vma=False
    )
```

```python
import functools
import math

import jax
import jax.numpy as jnp
from jax import lax
from jax.experimental import pallas as pl
from jax.sharding import Mesh
from jax.sharding import PartitionSpec as P

HEADS = 16


NORM_EPSILON = 1e-05

CLASS = ("z", "yh")
DEV = ("z", "yh", "core")


def rms_norm(values, gain):
    wide = values.astype(jnp.float32)
    factor = lax.rsqrt(jnp.mean(wide * wide, axis=-1, keepdims=True) + NORM_EPSILON)
    return (wide * factor * gain).astype(jnp.bfloat16)


def gather_rows(values, handler, by_permutes=False):
    count = lax.axis_size("group")
    if by_permutes:
        pieces = [values] + [
            lax.ppermute(values, "group", [(i, (i + shift) % count) for i in range(count)])
            for shift in range(1, count)
        ]
        own = lax.axis_index("group")
        order = (own - jnp.arange(count, dtype=jnp.int32)) % count
        gathered = jnp.take(jnp.stack(pieces), order, axis=0)
    else:
        copies = jnp.broadcast_to(values[None], (count,) + values.shape)
        gathered = lax.all_to_all(copies, "group", 0, 0, tiled=True)
    return handler(gathered.reshape(-1, values.shape[-1]), jnp.int32(0))


def scatter_sums(partial):
    count = lax.axis_size("group")
    pieces = partial.reshape(count, -1, partial.shape[-1])
    sent = lax.all_to_all(pieces.astype(jnp.bfloat16), "group", 0, 0, tiled=True)
    return jnp.sum(sent.astype(jnp.float32), axis=0)


def return_rows(columns):
    return lax.all_to_all(columns, "group", split_axis=0, concat_axis=1, tiled=True)


def projector(weight):

    def apply_rows(portion, offset):
        return jnp.dot(portion, weight, preferred_element_type=jnp.float32).astype(jnp.bfloat16)

    return apply_rows


def head_attention(queries, query_ids, prefix_keys, prefix_values, suffix_kv, suffix_ids, score_scale):
    prefix_scores = (
        jnp.einsum("bqd,kd->bqk", queries, prefix_keys, preferred_element_type=jnp.float32)
        * score_scale
    )
    near_scores = (
        jnp.einsum("bqd,bkd->bqk", queries, suffix_kv[:, :, 0], preferred_element_type=jnp.float32)
        * score_scale
    )
    allowed = query_ids[:, :, None] == suffix_ids[:, None, :]
    near_scores = jnp.where(allowed, near_scores, -jnp.inf)
    row_top = jnp.maximum(jnp.max(prefix_scores, axis=-1), jnp.max(near_scores, axis=-1))
    prefix_weights = jnp.exp(prefix_scores - row_top[:, :, None])
    near_weights = jnp.exp(near_scores - row_top[:, :, None])
    row_total = jnp.sum(prefix_weights, axis=-1) + jnp.sum(near_weights, axis=-1)
    mixed = jnp.einsum(
        "bqk,kd->bqd",
        prefix_weights.astype(jnp.bfloat16),
        prefix_values,
        preferred_element_type=jnp.float32,
    ) + jnp.einsum(
        "bqk,bkd->bqd",
        near_weights.astype(jnp.bfloat16),
        suffix_kv[:, :, 1],
        preferred_element_type=jnp.float32,
    )
    return (mixed / row_total[:, :, None]).astype(jnp.bfloat16)


def _attend_kernel(q_ref, pk_ref, pv_ref, nk_ref, nv_ref, bias_ref, o_ref, *, scale, sub):
    q = q_ref[...]
    dims = (((1,), (1,)), ((), ()))
    prefix_scores = jnp.dot(q, pk_ref[...], preferred_element_type=jnp.float32) * scale
    prefix_top = jnp.max(prefix_scores, axis=1, keepdims=True)
    for j in range(q.shape[0] // sub):
        rows = slice(j * sub, (j + 1) * sub)
        near_scores = (
            lax.dot_general(q[rows], nk_ref[j], dims, preferred_element_type=jnp.float32) * scale
            + bias_ref[j]
        )
        top = jnp.maximum(prefix_top[rows], jnp.max(near_scores, axis=1, keepdims=True))
        prefix_weights = jnp.exp(prefix_scores[rows] - top)
        near_weights = jnp.exp(near_scores - top)
        total = jnp.sum(prefix_weights, axis=1, keepdims=True) + jnp.sum(
            near_weights, axis=1, keepdims=True
        )
        mixed = jnp.dot(
            prefix_weights.astype(jnp.bfloat16), pv_ref[...], preferred_element_type=jnp.float32
        ) + jnp.dot(near_weights.astype(jnp.bfloat16), nv_ref[j], preferred_element_type=jnp.float32)
        o_ref[rows, :] = (mixed / total).astype(o_ref.dtype)


def attend(queries, prefix_keys_t, prefix_values, near_keys, near_values, bias, scale, block=256):
    rows, head_size = queries.shape
    sub = near_keys.shape[1] // 3
    per = block // sub
    keys_n = prefix_values.shape[0]
    near_n = near_keys.shape[1]
    return pl.pallas_call(
        functools.partial(_attend_kernel, scale=scale, sub=sub),
        grid=(rows // block,),
        in_specs=[
            pl.BlockSpec((block, head_size), lambda i: (i, 0)),
            pl.BlockSpec((head_size, keys_n), lambda i: (0, 0)),
            pl.BlockSpec((keys_n, head_size), lambda i: (0, 0)),
            pl.BlockSpec((per, near_n, head_size), lambda i: (i, 0, 0)),
            pl.BlockSpec((per, near_n, head_size), lambda i: (i, 0, 0)),
            pl.BlockSpec((per, sub, near_n), lambda i: (i, 0, 0)),
        ],
        out_specs=pl.BlockSpec((block, head_size), lambda i: (i, 0)),
        out_shape=jax.ShapeDtypeStruct((rows, head_size), queries.dtype),
    )(queries, prefix_keys_t, prefix_values, near_keys, near_values, bias)


def on_device(
    inputs,
    request,
    prefix_cache,
    norm1_gain,
    w_qkv,
    w_out,
    norm2_gain,
    w_gate,
    w_up,
    w_down,
    norm3_gain,
    w_next,
):
    tokens = inputs[0]
    tok_rows, model_width = tokens.shape
    head_count = HEADS
    head_size = model_width // head_count
    score_scale = 1.0 / math.sqrt(head_size)
    class_size = lax.axis_size(CLASS)
    core = lax.axis_index("core")
    cache = prefix_cache[0]
    cache_rows = cache.shape[0]
    prefix_kv = cache.reshape(cache_rows, 2, head_count, head_size).transpose(2, 1, 0, 3)
    normed_in = rms_norm(tokens, norm1_gain)
    projected = return_rows(gather_rows(normed_in, projector(w_qkv), by_permutes=True))
    own_qkv = projected.reshape(tok_rows, 3, head_count, head_size).transpose(2, 1, 0, 3)
    own_kv = jnp.concatenate([prefix_kv, own_qkv[:, 1:]], axis=2)
    payload = jnp.concatenate(
        [own_kv.reshape(head_count, -1, head_size), own_qkv[:, 0]], axis=1
    )
    received = lax.all_to_all(payload, CLASS, 0, 0, tiled=True)
    kv_rows = cache_rows + tok_rows
    class_kv = received[:, : 2 * kv_rows].reshape(class_size, 2, kv_rows, head_size)
    head_queries = received[:, 2 * kv_rows :]
    partner_kv = lax.ppermute(class_kv, "core", [(0, 1), (1, 0)])
    group_prefix = jnp.concatenate(
        [class_kv[:, :, :cache_rows], partner_kv[:, :, :cache_rows]], axis=0
    )
    prefix_keys = group_prefix[:, 0].reshape(-1, head_size)
    prefix_values = group_prefix[:, 1].reshape(-1, head_size)
    own_near = class_kv[:, :, cache_rows:]
    partner_near = partner_kv[:, :, cache_rows:]
    pad_kv = jnp.zeros((1,) + partner_near.shape[1:], partner_near.dtype)
    padded_kv = jnp.concatenate([pad_kv, partner_near, pad_kv], axis=0)
    before_kv = lax.dynamic_slice_in_dim(padded_kv, core, class_size, 0)
    after_kv = lax.dynamic_slice_in_dim(padded_kv, core + 1, class_size, 0)
    near_kv = jnp.concatenate([before_kv, own_near, after_kv], axis=2)
    dev_ids = request[0].reshape(2 * class_size, tok_rows)
    pad_ids = jnp.full((1, tok_rows), -1, jnp.int32)
    padded_ids = jnp.concatenate([pad_ids, dev_ids, pad_ids], axis=0)
    window = lax.dynamic_slice_in_dim(padded_ids, core, 2 * class_size + 1, 0)
    query_ids = window[1::2]
    near_ids = jnp.concatenate([window[0:-1:2], query_ids, window[2::2]], axis=1)
    bias = jnp.where(query_ids[:, :, None] == near_ids[:, None, :], 0.0, -jnp.inf)
    head_out = attend(
        head_queries.reshape(-1, head_size),
        prefix_keys.T,
        prefix_values,
        near_kv[:, 0],
        near_kv[:, 1],
        bias.astype(jnp.float32),
        score_scale,
    ).reshape(class_size, tok_rows, head_size)
    back = lax.all_to_all(head_out, CLASS, 0, 0, tiled=True)
    attended = back.transpose(1, 0, 2).reshape(tok_rows, model_width)
    after_attn = (
        tokens.astype(jnp.float32) + jnp.dot(attended, w_out, preferred_element_type=jnp.float32)
    ).astype(jnp.bfloat16)

    def expand(portion, offset):
        normed_mid = rms_norm(portion, norm2_gain)
        gate_proj = jnp.dot(normed_mid, w_gate, preferred_element_type=jnp.float32)
        up_proj = jnp.dot(normed_mid, w_up, preferred_element_type=jnp.float32)
        return (jax.nn.silu(gate_proj) * up_proj).astype(jnp.bfloat16)

    hidden = gather_rows(after_attn, expand)
    own_sums = scatter_sums(jnp.dot(hidden, w_down, preferred_element_type=jnp.float32))
    layer_out = (after_attn.astype(jnp.float32) + own_sums).astype(jnp.bfloat16)
    next_qkv = return_rows(gather_rows(rms_norm(layer_out, norm3_gain), projector(w_next)))
    return (attended[None], layer_out[None], next_qkv[None])


def solution(mesh):
    group_count, dev_count = mesh.devices.shape
    fine = Mesh(
        mesh.devices.reshape(group_count, dev_count // 4, 2, 2), ("group", "z", "yh", "core")
    )
    in_specs = (
        P("group", DEV, None),
        P("group", None),
        P("group", DEV, None),
        P(),
        P(None, "group"),
        P(),
        P(),
        P(None, "group"),
        P(None, "group"),
        P("group", None),
        P(),
        P(None, "group"),
    )
    out_specs = (P("group", DEV, None), P("group", DEV, None), P("group", DEV, None))
    return jax.shard_map(
        on_device, mesh=fine, in_specs=in_specs, out_specs=out_specs, check_vma=False
    )
```

```python
import functools
import math

import jax
import jax.numpy as jnp
from jax import lax
from jax.experimental import pallas as pl
from jax.sharding import Mesh
from jax.sharding import PartitionSpec as P

HEADS = 16


NORM_EPSILON = 1e-05

CLASS = ("z", "yh")
DEV = ("z", "yh", "core")


def rms_norm(values, gain):
    wide = values.astype(jnp.float32)
    factor = lax.rsqrt(jnp.mean(wide * wide, axis=-1, keepdims=True) + NORM_EPSILON)
    return (wide * factor * gain).astype(jnp.bfloat16)


def gather_rows(values, handler, by_permutes=False):
    count = lax.axis_size("group")
    if by_permutes:
        pieces = [values] + [
            lax.ppermute(values, "group", [(i, (i + shift) % count) for i in range(count)])
            for shift in range(1, count)
        ]
        own = lax.axis_index("group")
        order = (own - jnp.arange(count, dtype=jnp.int32)) % count
        gathered = jnp.take(jnp.stack(pieces), order, axis=0)
    else:
        copies = jnp.broadcast_to(values[None], (count,) + values.shape)
        gathered = lax.all_to_all(copies, "group", 0, 0, tiled=True)
    return handler(gathered.reshape(-1, values.shape[-1]), jnp.int32(0))


def scatter_sums(partial):
    count = lax.axis_size("group")
    pieces = partial.reshape(count, -1, partial.shape[-1])
    sent = lax.all_to_all(pieces.astype(jnp.bfloat16), "group", 0, 0, tiled=True)
    return jnp.sum(sent.astype(jnp.float32), axis=0)


def return_rows(columns):
    return lax.all_to_all(columns, "group", split_axis=0, concat_axis=1, tiled=True)


def projector(weight):

    def apply_rows(portion, offset):
        return jnp.dot(portion, weight, preferred_element_type=jnp.float32).astype(jnp.bfloat16)

    return apply_rows


def head_attention(queries, query_ids, prefix_keys, prefix_values, suffix_kv, suffix_ids, score_scale):
    prefix_scores = (
        jnp.einsum("bqd,kd->bqk", queries, prefix_keys, preferred_element_type=jnp.float32)
        * score_scale
    )
    near_scores = (
        jnp.einsum("bqd,bkd->bqk", queries, suffix_kv[:, :, 0], preferred_element_type=jnp.float32)
        * score_scale
    )
    allowed = query_ids[:, :, None] == suffix_ids[:, None, :]
    near_scores = jnp.where(allowed, near_scores, -jnp.inf)
    row_top = jnp.maximum(jnp.max(prefix_scores, axis=-1), jnp.max(near_scores, axis=-1))
    prefix_weights = jnp.exp(prefix_scores - row_top[:, :, None])
    near_weights = jnp.exp(near_scores - row_top[:, :, None])
    row_total = jnp.sum(prefix_weights, axis=-1) + jnp.sum(near_weights, axis=-1)
    mixed = jnp.einsum(
        "bqk,kd->bqd",
        prefix_weights.astype(jnp.bfloat16),
        prefix_values,
        preferred_element_type=jnp.float32,
    ) + jnp.einsum(
        "bqk,bkd->bqd",
        near_weights.astype(jnp.bfloat16),
        suffix_kv[:, :, 1],
        preferred_element_type=jnp.float32,
    )
    return (mixed / row_total[:, :, None]).astype(jnp.bfloat16)


def _attend_kernel(q_ref, pk_ref, pv_ref, nk_ref, nv_ref, bias_ref, o_ref, *, scale, sub):
    q = q_ref[...]
    dims = (((1,), (1,)), ((), ()))
    prefix_scores = jnp.dot(q, pk_ref[...], preferred_element_type=jnp.float32) * scale
    prefix_top = jnp.max(prefix_scores, axis=1, keepdims=True)
    for j in range(q.shape[0] // sub):
        rows = slice(j * sub, (j + 1) * sub)
        near_scores = (
            lax.dot_general(q[rows], nk_ref[j], dims, preferred_element_type=jnp.float32) * scale
            + bias_ref[j]
        )
        top = jnp.maximum(prefix_top[rows], jnp.max(near_scores, axis=1, keepdims=True))
        prefix_weights = jnp.exp(prefix_scores[rows] - top)
        near_weights = jnp.exp(near_scores - top)
        total = jnp.sum(prefix_weights, axis=1, keepdims=True) + jnp.sum(
            near_weights, axis=1, keepdims=True
        )
        mixed = jnp.dot(
            prefix_weights.astype(jnp.bfloat16), pv_ref[...], preferred_element_type=jnp.float32
        ) + jnp.dot(near_weights.astype(jnp.bfloat16), nv_ref[j], preferred_element_type=jnp.float32)
        o_ref[rows, :] = (mixed / total).astype(o_ref.dtype)


def attend(queries, prefix_keys_t, prefix_values, near_keys, near_values, bias, scale, block=256):
    rows, head_size = queries.shape
    sub = near_keys.shape[1] // 3
    per = block // sub
    keys_n = prefix_values.shape[0]
    near_n = near_keys.shape[1]
    return pl.pallas_call(
        functools.partial(_attend_kernel, scale=scale, sub=sub),
        grid=(rows // block,),
        in_specs=[
            pl.BlockSpec((block, head_size), lambda i: (i, 0)),
            pl.BlockSpec((head_size, keys_n), lambda i: (0, 0)),
            pl.BlockSpec((keys_n, head_size), lambda i: (0, 0)),
            pl.BlockSpec((per, near_n, head_size), lambda i: (i, 0, 0)),
            pl.BlockSpec((per, near_n, head_size), lambda i: (i, 0, 0)),
            pl.BlockSpec((per, sub, near_n), lambda i: (i, 0, 0)),
        ],
        out_specs=pl.BlockSpec((block, head_size), lambda i: (i, 0)),
        out_shape=jax.ShapeDtypeStruct((rows, head_size), queries.dtype),
    )(queries, prefix_keys_t, prefix_values, near_keys, near_values, bias)


def on_device(
    inputs,
    request,
    prefix_cache,
    norm1_gain,
    w_qkv,
    w_out,
    norm2_gain,
    w_gate,
    w_up,
    w_down,
    norm3_gain,
    w_next,
):
    tokens = inputs[0]
    tok_rows, model_width = tokens.shape
    head_count = HEADS
    head_size = model_width // head_count
    score_scale = 1.0 / math.sqrt(head_size)
    class_size = lax.axis_size(CLASS)
    core = lax.axis_index("core")
    cache = prefix_cache[0]
    cache_rows = cache.shape[0]
    prefix_kv = cache.reshape(cache_rows, 2, head_count, head_size).transpose(2, 1, 0, 3)
    class_prefix = lax.all_to_all(prefix_kv, CLASS, 0, 0, tiled=True)
    partner_prefix = lax.ppermute(class_prefix, "core", [(0, 1), (1, 0)])
    group_prefix = jnp.concatenate([class_prefix, partner_prefix], axis=0)
    prefix_keys = group_prefix[:, 0].reshape(-1, head_size)
    prefix_values = group_prefix[:, 1].reshape(-1, head_size)
    normed_in = rms_norm(tokens, norm1_gain)
    projected = return_rows(gather_rows(normed_in, projector(w_qkv), by_permutes=True))
    own_qkv = projected.reshape(tok_rows, 3, head_count, head_size).transpose(2, 0, 1, 3)
    class_qkv = lax.all_to_all(own_qkv, CLASS, 0, 0, tiled=True)
    head_queries = class_qkv[:, :, 0]
    class_kv = class_qkv[:, :, 1:]
    partner_kv = lax.ppermute(class_kv, "core", [(0, 1), (1, 0)])
    pad_kv = jnp.zeros((1,) + partner_kv.shape[1:], partner_kv.dtype)
    padded_kv = jnp.concatenate([pad_kv, partner_kv, pad_kv], axis=0)
    before_kv = lax.dynamic_slice_in_dim(padded_kv, core, class_size, 0)
    after_kv = lax.dynamic_slice_in_dim(padded_kv, core + 1, class_size, 0)
    near_kv = jnp.concatenate([before_kv, class_kv, after_kv], axis=1)
    dev_ids = request[0].reshape(2 * class_size, tok_rows)
    pad_ids = jnp.full((1, tok_rows), -1, jnp.int32)
    padded_ids = jnp.concatenate([pad_ids, dev_ids, pad_ids], axis=0)
    window = lax.dynamic_slice_in_dim(padded_ids, core, 2 * class_size + 1, 0)
    query_ids = window[1::2]
    near_ids = jnp.concatenate([window[0:-1:2], query_ids, window[2::2]], axis=1)
    bias = jnp.where(query_ids[:, :, None] == near_ids[:, None, :], 0.0, -jnp.inf)
    head_out = attend(
        head_queries.reshape(-1, head_size),
        prefix_keys.T,
        prefix_values,
        near_kv[:, :, 0],
        near_kv[:, :, 1],
        bias.astype(jnp.float32),
        score_scale,
    ).reshape(class_size, tok_rows, head_size)
    back = lax.all_to_all(head_out, CLASS, 0, 0, tiled=True)
    attended = back.transpose(1, 0, 2).reshape(tok_rows, model_width)
    after_attn = (
        tokens.astype(jnp.float32) + jnp.dot(attended, w_out, preferred_element_type=jnp.float32)
    ).astype(jnp.bfloat16)

    def expand(portion, offset):
        normed_mid = rms_norm(portion, norm2_gain)
        gate_proj = jnp.dot(normed_mid, w_gate, preferred_element_type=jnp.float32)
        up_proj = jnp.dot(normed_mid, w_up, preferred_element_type=jnp.float32)
        return (jax.nn.silu(gate_proj) * up_proj).astype(jnp.bfloat16)

    hidden = gather_rows(after_attn, expand, by_permutes=True)
    own_sums = scatter_sums(jnp.dot(hidden, w_down, preferred_element_type=jnp.float32))
    layer_out = (after_attn.astype(jnp.float32) + own_sums).astype(jnp.bfloat16)
    next_qkv = return_rows(
        gather_rows(rms_norm(layer_out, norm3_gain), projector(w_next), by_permutes=True)
    )
    return (attended[None], layer_out[None], next_qkv[None])


def solution(mesh):
    group_count, dev_count = mesh.devices.shape
    fine = Mesh(
        mesh.devices.reshape(group_count, dev_count // 4, 2, 2), ("group", "z", "yh", "core")
    )
    in_specs = (
        P("group", DEV, None),
        P("group", None),
        P("group", DEV, None),
        P(),
        P(None, "group"),
        P(),
        P(),
        P(None, "group"),
        P(None, "group"),
        P("group", None),
        P(),
        P(None, "group"),
    )
    out_specs = (P("group", DEV, None), P("group", DEV, None), P("group", DEV, None))
    return jax.shard_map(
        on_device, mesh=fine, in_specs=in_specs, out_specs=out_specs, check_vma=False
    )
```

```python
import functools
import math

import jax
import jax.numpy as jnp
from jax import lax
from jax.experimental import pallas as pl
from jax.sharding import Mesh
from jax.sharding import PartitionSpec as P

HEADS = 16


NORM_EPSILON = 1e-05

CLASS = ("z", "yh")
DEV = ("z", "yh", "core")


def rms_norm(values, gain):
    wide = values.astype(jnp.float32)
    factor = lax.rsqrt(jnp.mean(wide * wide, axis=-1, keepdims=True) + NORM_EPSILON)
    return (wide * factor * gain).astype(jnp.bfloat16)


def gather_rows(values, handler, by_permutes=False):
    count = lax.axis_size("group")
    if by_permutes:
        pieces = [values] + [
            lax.ppermute(values, "group", [(i, (i + shift) % count) for i in range(count)])
            for shift in range(1, count)
        ]
        own = lax.axis_index("group")
        order = (own - jnp.arange(count, dtype=jnp.int32)) % count
        gathered = jnp.take(jnp.stack(pieces), order, axis=0)
    else:
        copies = jnp.broadcast_to(values[None], (count,) + values.shape)
        gathered = lax.all_to_all(copies, "group", 0, 0, tiled=True)
    return handler(gathered.reshape(-1, values.shape[-1]), jnp.int32(0))


def scatter_sums(partial):
    count = lax.axis_size("group")
    pieces = partial.reshape(count, -1, partial.shape[-1])
    sent = lax.all_to_all(pieces.astype(jnp.bfloat16), "group", 0, 0, tiled=True)
    return jnp.sum(sent.astype(jnp.float32), axis=0)


def return_rows(columns):
    return lax.all_to_all(columns, "group", split_axis=0, concat_axis=1, tiled=True)


def projector(weight):

    def apply_rows(portion, offset):
        return jnp.dot(portion, weight, preferred_element_type=jnp.float32).astype(jnp.bfloat16)

    return apply_rows


def head_attention(queries, query_ids, prefix_keys, prefix_values, suffix_kv, suffix_ids, score_scale):
    prefix_scores = (
        jnp.einsum("bqd,kd->bqk", queries, prefix_keys, preferred_element_type=jnp.float32)
        * score_scale
    )
    near_scores = (
        jnp.einsum("bqd,bkd->bqk", queries, suffix_kv[:, :, 0], preferred_element_type=jnp.float32)
        * score_scale
    )
    allowed = query_ids[:, :, None] == suffix_ids[:, None, :]
    near_scores = jnp.where(allowed, near_scores, -jnp.inf)
    row_top = jnp.maximum(jnp.max(prefix_scores, axis=-1), jnp.max(near_scores, axis=-1))
    prefix_weights = jnp.exp(prefix_scores - row_top[:, :, None])
    near_weights = jnp.exp(near_scores - row_top[:, :, None])
    row_total = jnp.sum(prefix_weights, axis=-1) + jnp.sum(near_weights, axis=-1)
    mixed = jnp.einsum(
        "bqk,kd->bqd",
        prefix_weights.astype(jnp.bfloat16),
        prefix_values,
        preferred_element_type=jnp.float32,
    ) + jnp.einsum(
        "bqk,bkd->bqd",
        near_weights.astype(jnp.bfloat16),
        suffix_kv[:, :, 1],
        preferred_element_type=jnp.float32,
    )
    return (mixed / row_total[:, :, None]).astype(jnp.bfloat16)


def _attend_kernel(q_ref, pk_ref, pv_ref, nk_ref, nv_ref, bias_ref, o_ref, *, scale, sub):
    q = q_ref[...]
    dims = (((1,), (1,)), ((), ()))
    prefix_scores = jnp.dot(q, pk_ref[...], preferred_element_type=jnp.float32) * scale
    prefix_top = jnp.max(prefix_scores, axis=1, keepdims=True)
    for j in range(q.shape[0] // sub):
        rows = slice(j * sub, (j + 1) * sub)
        near_scores = (
            lax.dot_general(q[rows], nk_ref[j], dims, preferred_element_type=jnp.float32) * scale
            + bias_ref[j]
        )
        top = jnp.maximum(prefix_top[rows], jnp.max(near_scores, axis=1, keepdims=True))
        prefix_weights = jnp.exp(prefix_scores[rows] - top)
        near_weights = jnp.exp(near_scores - top)
        total = jnp.sum(prefix_weights, axis=1, keepdims=True) + jnp.sum(
            near_weights, axis=1, keepdims=True
        )
        mixed = jnp.dot(
            prefix_weights.astype(jnp.bfloat16), pv_ref[...], preferred_element_type=jnp.float32
        ) + jnp.dot(near_weights.astype(jnp.bfloat16), nv_ref[j], preferred_element_type=jnp.float32)
        o_ref[rows, :] = (mixed / total).astype(o_ref.dtype)


def attend(queries, prefix_keys_t, prefix_values, near_keys, near_values, bias, scale, block=256):
    rows, head_size = queries.shape
    sub = near_keys.shape[1] // 3
    per = block // sub
    keys_n = prefix_values.shape[0]
    near_n = near_keys.shape[1]
    return pl.pallas_call(
        functools.partial(_attend_kernel, scale=scale, sub=sub),
        grid=(rows // block,),
        in_specs=[
            pl.BlockSpec((block, head_size), lambda i: (i, 0)),
            pl.BlockSpec((head_size, keys_n), lambda i: (0, 0)),
            pl.BlockSpec((keys_n, head_size), lambda i: (0, 0)),
            pl.BlockSpec((per, near_n, head_size), lambda i: (i, 0, 0)),
            pl.BlockSpec((per, near_n, head_size), lambda i: (i, 0, 0)),
            pl.BlockSpec((per, sub, near_n), lambda i: (i, 0, 0)),
        ],
        out_specs=pl.BlockSpec((block, head_size), lambda i: (i, 0)),
        out_shape=jax.ShapeDtypeStruct((rows, head_size), queries.dtype),
    )(queries, prefix_keys_t, prefix_values, near_keys, near_values, bias)


def on_device(
    inputs,
    request,
    prefix_cache,
    norm1_gain,
    w_qkv,
    w_out,
    norm2_gain,
    w_gate,
    w_up,
    w_down,
    norm3_gain,
    w_next,
):
    tokens = inputs[0]
    tok_rows, model_width = tokens.shape
    head_count = HEADS
    head_size = model_width // head_count
    score_scale = 1.0 / math.sqrt(head_size)
    class_size = lax.axis_size(CLASS)
    core = lax.axis_index("core")
    cache = prefix_cache[0]
    cache_rows = cache.shape[0]
    prefix_kv = cache.reshape(cache_rows, 2, head_count, head_size).transpose(2, 1, 0, 3)
    class_prefix = lax.all_to_all(prefix_kv, CLASS, 0, 0, tiled=True)
    partner_prefix = lax.ppermute(class_prefix, "core", [(0, 1), (1, 0)])
    group_prefix = jnp.concatenate([class_prefix, partner_prefix], axis=0)
    prefix_keys = group_prefix[:, 0].reshape(-1, head_size)
    prefix_values = group_prefix[:, 1].reshape(-1, head_size)
    normed_in, class_prefix = lax.optimization_barrier((rms_norm(tokens, norm1_gain), class_prefix))
    projected = return_rows(gather_rows(normed_in, projector(w_qkv), by_permutes=True))
    own_qkv = projected.reshape(tok_rows, 3, head_count, head_size).transpose(2, 0, 1, 3)
    class_qkv = lax.all_to_all(own_qkv, CLASS, 0, 0, tiled=True)
    head_queries = class_qkv[:, :, 0]
    class_kv = class_qkv[:, :, 1:]
    partner_kv = lax.ppermute(class_kv, "core", [(0, 1), (1, 0)])
    pad_kv = jnp.zeros((1,) + partner_kv.shape[1:], partner_kv.dtype)
    padded_kv = jnp.concatenate([pad_kv, partner_kv, pad_kv], axis=0)
    before_kv = lax.dynamic_slice_in_dim(padded_kv, core, class_size, 0)
    after_kv = lax.dynamic_slice_in_dim(padded_kv, core + 1, class_size, 0)
    near_kv = jnp.concatenate([before_kv, class_kv, after_kv], axis=1)
    dev_ids = request[0].reshape(2 * class_size, tok_rows)
    pad_ids = jnp.full((1, tok_rows), -1, jnp.int32)
    padded_ids = jnp.concatenate([pad_ids, dev_ids, pad_ids], axis=0)
    window = lax.dynamic_slice_in_dim(padded_ids, core, 2 * class_size + 1, 0)
    query_ids = window[1::2]
    near_ids = jnp.concatenate([window[0:-1:2], query_ids, window[2::2]], axis=1)
    bias = jnp.where(query_ids[:, :, None] == near_ids[:, None, :], 0.0, -jnp.inf)
    head_out = attend(
        head_queries.reshape(-1, head_size),
        prefix_keys.T,
        prefix_values,
        near_kv[:, :, 0],
        near_kv[:, :, 1],
        bias.astype(jnp.float32),
        score_scale,
    ).reshape(class_size, tok_rows, head_size)
    back = lax.all_to_all(head_out, CLASS, 0, 0, tiled=True)
    attended = back.transpose(1, 0, 2).reshape(tok_rows, model_width)
    after_attn = (
        tokens.astype(jnp.float32) + jnp.dot(attended, w_out, preferred_element_type=jnp.float32)
    ).astype(jnp.bfloat16)

    def expand(portion, offset):
        normed_mid = rms_norm(portion, norm2_gain)
        gate_proj = jnp.dot(normed_mid, w_gate, preferred_element_type=jnp.float32)
        up_proj = jnp.dot(normed_mid, w_up, preferred_element_type=jnp.float32)
        return (jax.nn.silu(gate_proj) * up_proj).astype(jnp.bfloat16)

    hidden = gather_rows(after_attn, expand)
    own_sums = scatter_sums(jnp.dot(hidden, w_down, preferred_element_type=jnp.float32))
    layer_out = (after_attn.astype(jnp.float32) + own_sums).astype(jnp.bfloat16)
    next_qkv = return_rows(gather_rows(rms_norm(layer_out, norm3_gain), projector(w_next)))
    return (attended[None], layer_out[None], next_qkv[None])


def solution(mesh):
    group_count, dev_count = mesh.devices.shape
    fine = Mesh(
        mesh.devices.reshape(group_count, dev_count // 4, 2, 2), ("group", "z", "yh", "core")
    )
    in_specs = (
        P("group", DEV, None),
        P("group", None),
        P("group", DEV, None),
        P(),
        P(None, "group"),
        P(),
        P(),
        P(None, "group"),
        P(None, "group"),
        P("group", None),
        P(),
        P(None, "group"),
    )
    out_specs = (P("group", DEV, None), P("group", DEV, None), P("group", DEV, None))
    return jax.shard_map(
        on_device, mesh=fine, in_specs=in_specs, out_specs=out_specs, check_vma=False
    )
```

```python
import functools
import math

import jax
import jax.numpy as jnp
from jax import lax
from jax.experimental import pallas as pl
from jax.sharding import Mesh
from jax.sharding import PartitionSpec as P

HEADS = 16


NORM_EPSILON = 1e-05

CLASS = ("z", "yh")
DEV = ("z", "yh", "core")


def rms_norm(values, gain):
    wide = values.astype(jnp.float32)
    factor = lax.rsqrt(jnp.mean(wide * wide, axis=-1, keepdims=True) + NORM_EPSILON)
    return (wide * factor * gain).astype(jnp.bfloat16)


def gather_rows(values, handler, by_permutes=False):
    count = lax.axis_size("group")
    if by_permutes:
        pieces = [values] + [
            lax.ppermute(values, "group", [(i, (i + shift) % count) for i in range(count)])
            for shift in range(1, count)
        ]
        own = lax.axis_index("group")
        order = (own - jnp.arange(count, dtype=jnp.int32)) % count
        gathered = jnp.take(jnp.stack(pieces), order, axis=0)
    else:
        copies = jnp.broadcast_to(values[None], (count,) + values.shape)
        gathered = lax.all_to_all(copies, "group", 0, 0, tiled=True)
    return handler(gathered.reshape(-1, values.shape[-1]), jnp.int32(0))


def scatter_sums(partial):
    count = lax.axis_size("group")
    pieces = partial.reshape(count, -1, partial.shape[-1])
    sent = lax.all_to_all(pieces.astype(jnp.bfloat16), "group", 0, 0, tiled=True)
    return jnp.sum(sent.astype(jnp.float32), axis=0)


def return_rows(columns):
    return lax.all_to_all(columns, "group", split_axis=0, concat_axis=1, tiled=True)


def projector(weight):

    def apply_rows(portion, offset):
        return jnp.dot(portion, weight, preferred_element_type=jnp.float32).astype(jnp.bfloat16)

    return apply_rows


def head_attention(queries, query_ids, prefix_keys, prefix_values, suffix_kv, suffix_ids, score_scale):
    prefix_scores = (
        jnp.einsum("bqd,kd->bqk", queries, prefix_keys, preferred_element_type=jnp.float32)
        * score_scale
    )
    near_scores = (
        jnp.einsum("bqd,bkd->bqk", queries, suffix_kv[:, :, 0], preferred_element_type=jnp.float32)
        * score_scale
    )
    allowed = query_ids[:, :, None] == suffix_ids[:, None, :]
    near_scores = jnp.where(allowed, near_scores, -jnp.inf)
    row_top = jnp.maximum(jnp.max(prefix_scores, axis=-1), jnp.max(near_scores, axis=-1))
    prefix_weights = jnp.exp(prefix_scores - row_top[:, :, None])
    near_weights = jnp.exp(near_scores - row_top[:, :, None])
    row_total = jnp.sum(prefix_weights, axis=-1) + jnp.sum(near_weights, axis=-1)
    mixed = jnp.einsum(
        "bqk,kd->bqd",
        prefix_weights.astype(jnp.bfloat16),
        prefix_values,
        preferred_element_type=jnp.float32,
    ) + jnp.einsum(
        "bqk,bkd->bqd",
        near_weights.astype(jnp.bfloat16),
        suffix_kv[:, :, 1],
        preferred_element_type=jnp.float32,
    )
    return (mixed / row_total[:, :, None]).astype(jnp.bfloat16)


def _attend_kernel(q_ref, pk_ref, pv_ref, nk_ref, nv_ref, bias_ref, o_ref, *, scale, sub):
    q = q_ref[...]
    dims = (((1,), (1,)), ((), ()))
    prefix_scores = jnp.dot(q, pk_ref[...], preferred_element_type=jnp.float32) * scale
    prefix_top = jnp.max(prefix_scores, axis=1, keepdims=True)
    for j in range(q.shape[0] // sub):
        rows = slice(j * sub, (j + 1) * sub)
        near_scores = (
            lax.dot_general(q[rows], nk_ref[j], dims, preferred_element_type=jnp.float32) * scale
            + bias_ref[j]
        )
        top = jnp.maximum(prefix_top[rows], jnp.max(near_scores, axis=1, keepdims=True))
        prefix_weights = jnp.exp(prefix_scores[rows] - top)
        near_weights = jnp.exp(near_scores - top)
        total = jnp.sum(prefix_weights, axis=1, keepdims=True) + jnp.sum(
            near_weights, axis=1, keepdims=True
        )
        mixed = jnp.dot(
            prefix_weights.astype(jnp.bfloat16), pv_ref[...], preferred_element_type=jnp.float32
        ) + jnp.dot(near_weights.astype(jnp.bfloat16), nv_ref[j], preferred_element_type=jnp.float32)
        o_ref[rows, :] = (mixed / total).astype(o_ref.dtype)


def attend(queries, prefix_keys_t, prefix_values, near_keys, near_values, bias, scale, block=512):
    rows, head_size = queries.shape
    sub = near_keys.shape[1] // 3
    per = block // sub
    keys_n = prefix_values.shape[0]
    near_n = near_keys.shape[1]
    return pl.pallas_call(
        functools.partial(_attend_kernel, scale=scale, sub=sub),
        grid=(rows // block,),
        in_specs=[
            pl.BlockSpec((block, head_size), lambda i: (i, 0)),
            pl.BlockSpec((head_size, keys_n), lambda i: (0, 0)),
            pl.BlockSpec((keys_n, head_size), lambda i: (0, 0)),
            pl.BlockSpec((per, near_n, head_size), lambda i: (i, 0, 0)),
            pl.BlockSpec((per, near_n, head_size), lambda i: (i, 0, 0)),
            pl.BlockSpec((per, sub, near_n), lambda i: (i, 0, 0)),
        ],
        out_specs=pl.BlockSpec((block, head_size), lambda i: (i, 0)),
        out_shape=jax.ShapeDtypeStruct((rows, head_size), queries.dtype),
    )(queries, prefix_keys_t, prefix_values, near_keys, near_values, bias)


def on_device(
    inputs,
    request,
    prefix_cache,
    norm1_gain,
    w_qkv,
    w_out,
    norm2_gain,
    w_gate,
    w_up,
    w_down,
    norm3_gain,
    w_next,
):
    tokens = inputs[0]
    tok_rows, model_width = tokens.shape
    head_count = HEADS
    head_size = model_width // head_count
    score_scale = 1.0 / math.sqrt(head_size)
    class_size = lax.axis_size(CLASS)
    core = lax.axis_index("core")
    cache = prefix_cache[0]
    cache_rows = cache.shape[0]
    prefix_kv = cache.reshape(cache_rows, 2, head_count, head_size).transpose(2, 1, 0, 3)
    class_prefix = lax.all_to_all(prefix_kv, CLASS, 0, 0, tiled=True)
    partner_prefix = lax.ppermute(class_prefix, "core", [(0, 1), (1, 0)])
    group_prefix = jnp.concatenate([class_prefix, partner_prefix], axis=0)
    prefix_keys = group_prefix[:, 0].reshape(-1, head_size)
    prefix_values = group_prefix[:, 1].reshape(-1, head_size)
    normed_in = rms_norm(tokens, norm1_gain)
    projected = return_rows(gather_rows(normed_in, projector(w_qkv), by_permutes=True))
    own_qkv = projected.reshape(tok_rows, 3, head_count, head_size).transpose(2, 0, 1, 3)
    class_qkv = lax.all_to_all(own_qkv, CLASS, 0, 0, tiled=True)
    head_queries = class_qkv[:, :, 0]
    class_kv = class_qkv[:, :, 1:]
    partner_kv = lax.ppermute(class_kv, "core", [(0, 1), (1, 0)])
    pad_kv = jnp.zeros((1,) + partner_kv.shape[1:], partner_kv.dtype)
    padded_kv = jnp.concatenate([pad_kv, partner_kv, pad_kv], axis=0)
    before_kv = lax.dynamic_slice_in_dim(padded_kv, core, class_size, 0)
    after_kv = lax.dynamic_slice_in_dim(padded_kv, core + 1, class_size, 0)
    near_kv = jnp.concatenate([before_kv, class_kv, after_kv], axis=1)
    dev_ids = request[0].reshape(2 * class_size, tok_rows)
    pad_ids = jnp.full((1, tok_rows), -1, jnp.int32)
    padded_ids = jnp.concatenate([pad_ids, dev_ids, pad_ids], axis=0)
    window = lax.dynamic_slice_in_dim(padded_ids, core, 2 * class_size + 1, 0)
    query_ids = window[1::2]
    near_ids = jnp.concatenate([window[0:-1:2], query_ids, window[2::2]], axis=1)
    bias = jnp.where(query_ids[:, :, None] == near_ids[:, None, :], 0.0, -jnp.inf)
    head_out = attend(
        head_queries.reshape(-1, head_size),
        prefix_keys.T,
        prefix_values,
        near_kv[:, :, 0],
        near_kv[:, :, 1],
        bias.astype(jnp.float32),
        score_scale,
    ).reshape(class_size, tok_rows, head_size)
    back = lax.all_to_all(head_out, CLASS, 0, 0, tiled=True)
    attended = back.transpose(1, 0, 2).reshape(tok_rows, model_width)
    after_attn = (
        tokens.astype(jnp.float32) + jnp.dot(attended, w_out, preferred_element_type=jnp.float32)
    ).astype(jnp.bfloat16)

    def expand(portion, offset):
        normed_mid = rms_norm(portion, norm2_gain)
        gate_proj = jnp.dot(normed_mid, w_gate, preferred_element_type=jnp.float32)
        up_proj = jnp.dot(normed_mid, w_up, preferred_element_type=jnp.float32)
        return (jax.nn.silu(gate_proj) * up_proj).astype(jnp.bfloat16)

    hidden = gather_rows(after_attn, expand)
    own_sums = scatter_sums(jnp.dot(hidden, w_down, preferred_element_type=jnp.float32))
    layer_out = (after_attn.astype(jnp.float32) + own_sums).astype(jnp.bfloat16)
    next_qkv = return_rows(gather_rows(rms_norm(layer_out, norm3_gain), projector(w_next)))
    return (attended[None], layer_out[None], next_qkv[None])


def solution(mesh):
    group_count, dev_count = mesh.devices.shape
    fine = Mesh(
        mesh.devices.reshape(group_count, dev_count // 4, 2, 2), ("group", "z", "yh", "core")
    )
    in_specs = (
        P("group", DEV, None),
        P("group", None),
        P("group", DEV, None),
        P(),
        P(None, "group"),
        P(),
        P(),
        P(None, "group"),
        P(None, "group"),
        P("group", None),
        P(),
        P(None, "group"),
    )
    out_specs = (P("group", DEV, None), P("group", DEV, None), P("group", DEV, None))
    return jax.shard_map(
        on_device, mesh=fine, in_specs=in_specs, out_specs=out_specs, check_vma=False
    )
```
